256 devices in a mesh: uly: 8 (over x_hi, y), blk: 32 (over x_lo, z, core).
Axes of the slice: x: 4 (x_hi: 2, x_lo: 2; x = x_hi * 2 + x_lo), y: 4, z: 8, core: 2. Of those that a mesh axis runs over, the one named last changes fastest.
Arguments:
- queries: bfloat16 [16384, 2048], P(('uly', 'blk')), may hold values from -6 to 6
- key_vector_rows: bfloat16 [16384, 256], P(('uly', 'blk')), may hold values from -6 to 6
- value_vector_rows: bfloat16 [16384, 256], P(('uly', 'blk')), may hold values from -6 to 6
- out_grad: bfloat16 [16384, 2048], P(('uly', 'blk')), may hold values from -6 to 6
- block_list: int32 [16, 128, 8], P('uly'), may hold values from 0 to 127, as said below
Outputs:
- attended: bfloat16 [16384, 2048], P(('uly', 'blk'))
- query_grad: bfloat16 [16384, 2048], P(('uly', 'blk'))
- gradient_keys: bfloat16 [16384, 256], P(('uly', 'blk'))
- gradient_values: bfloat16 [16384, 256], P(('uly', 'blk'))
The draws below stay inside these ranges and needn't reach their ends.
Inputs may be any that keep to these rules, and one draw needn't show every extreme that they name: block_list[h, i] names key blocks for query block i of head h: its first entry is always i itself, every entry is at most i, and a block may be named several times.
All inputs are finite; a program needn't handle non-finite values.
Results may differ from the reference program's by a relative error of at most 0.039.
Values may be sent and summed in bfloat16 or wider, within the bound.
No kernel may reach another device: no remote copies, remote signals or barrier semaphores. Data moves between devices by JAX's collectives and lax.ppermute only.
A program may use at most 128 MiB of HBM per device.

```python
import math
import jax
import jax.numpy as jnp
from jax import lax

QUERY_HEADS = 16
KEY_VALUE_HEADS = 2
HEAD_SIZE = 128
BLOCK = 128
KMAX = 8
SEQUENCE_TOKENS = 16384
NB = 128


def draw_queries(key, part):
    sampled_values = jax.random.normal(jax.random.fold_in(key, 21), (SEQUENCE_TOKENS, QUERY_HEADS, HEAD_SIZE), jnp.float32)
    return jnp.clip(sampled_values, -6.0, 6.0).reshape(SEQUENCE_TOKENS, QUERY_HEADS * HEAD_SIZE).astype(jnp.bfloat16)


def draw_key_vector_rows(key, part):
    sampled_values = jax.random.normal(jax.random.fold_in(key, 22), (SEQUENCE_TOKENS, KEY_VALUE_HEADS, HEAD_SIZE), jnp.float32)
    return jnp.clip(sampled_values, -6.0, 6.0).reshape(SEQUENCE_TOKENS, KEY_VALUE_HEADS * HEAD_SIZE).astype(jnp.bfloat16)


def draw_block_list(key, part):
    first_key = jax.random.fold_in(key, 31)
    second_key = jax.random.fold_in(key, 32)
    third_key = jax.random.fold_in(key, 33)
    row_ids = jnp.arange(NB, dtype=jnp.int32)[:, None]
    col_ids = jnp.arange(NB, dtype=jnp.int32)[None, :]
    ranking = jax.random.randint(first_key, (QUERY_HEADS, NB, NB), 0, 1 << 20) * NB + col_ids
    ranking = jnp.where(col_ids == row_ids, 1 << 30, ranking)
    ranking = jnp.where(col_ids > row_ids, -1 - col_ids, ranking)
    chosen = lax.top_k(ranking, KMAX)[1].astype(jnp.int32)
    head_cap = jax.random.randint(second_key, (QUERY_HEADS, 1), 2, KMAX + 1)
    counts = jax.random.randint(third_key, (QUERY_HEADS, NB), 1, KMAX + 1)
    counts = jnp.minimum(jnp.minimum(counts, head_cap), row_ids[:, 0][None, :] + 1)
    slot_ids = jnp.arange(KMAX, dtype=jnp.int32)
    diagonal = jnp.broadcast_to(row_ids[None, :, :], (QUERY_HEADS, NB, KMAX))
    return jnp.where(slot_ids[None, None, :] < counts[:, :, None], chosen, diagonal).astype(jnp.int32)


def level_of(key, shape, shards, smallest, top_value):
    factor_of = 1.0
    for axis_at, blocks in shards:
        steps = jax.random.uniform(jax.random.fold_in(jax.random.fold_in(key, 6), axis_at), (blocks,), jnp.float32, smallest / len(shards), top_value / len(shards))
        factor_of = factor_of * jnp.repeat(jnp.exp(steps), shape[axis_at] // blocks).reshape((-1,) + (1,) * (len(shape) - 1 - axis_at))
    return factor_of


def centred(key, dims, width, limit, cuts=(), kind=jnp.bfloat16):
    level = level_of(key, dims, cuts, -0.22, 0.18) if cuts else 1.0
    result = jax.random.normal(key, dims, jnp.float32) * width * level
    return jnp.minimum(jnp.maximum(result, -limit), limit).astype(kind)


def setup_inputs(seed: int = 0) -> dict:
    seeds = jax.random.split(jax.random.key(seed), 6)
    return {
        "queries": draw_queries(jax.random.fold_in(seeds[5], 71), 0),
        "key_vector_rows": draw_key_vector_rows(jax.random.fold_in(seeds[5], 71), 0),
        "value_vector_rows": centred(seeds[2], (SEQUENCE_TOKENS, KEY_VALUE_HEADS * HEAD_SIZE), 1.0, 6.0, ((0, 256),)),
        "out_grad": centred(seeds[3], (SEQUENCE_TOKENS, QUERY_HEADS * HEAD_SIZE), 1.0, 6.0, ((0, 256),)),
        "block_list": draw_block_list(jax.random.fold_in(seeds[5], 71), 0),
    }


def head_pass(head_index, queries3, keys_by_head, values_by_head, grads3, block_list):
    query_group_width = QUERY_HEADS // KEY_VALUE_HEADS
    query_head = queries3[head_index]
    key_head = keys_by_head[head_index // query_group_width]
    value_head = values_by_head[head_index // query_group_width]
    grad_head = grads3[head_index]
    lists_head = block_list[head_index]
    score_scale = 1.0 / math.sqrt(HEAD_SIZE)
    offsets = jnp.arange(BLOCK, dtype=jnp.int32)
    earlier = jnp.arange(KMAX)[:, None] > jnp.arange(KMAX)[None, :]

    def block_step(sums_pair, block_index):
        key_acc, value_acc = sums_pair
        first_row = block_index * BLOCK
        query_block = lax.dynamic_slice_in_dim(query_head, first_row, BLOCK, 0)
        grad_block = lax.dynamic_slice_in_dim(grad_head, first_row, BLOCK, 0)
        entries = lists_head[block_index]
        repeated = jnp.any((entries[:, None] == entries[None, :]) & earlier, axis=1)
        positions = (entries[:, None] * BLOCK + offsets[None, :]).reshape(-1).astype(jnp.int32)
        live_keys = jnp.repeat(jnp.logical_not(repeated), BLOCK)
        query_pos = first_row + offsets
        allowed = (positions[None, :] <= query_pos[:, None]) & live_keys[None, :]
        key_block = key_head[positions]
        value_block = value_head[positions]
        scores = jnp.dot(query_block, key_block.T, preferred_element_type=jnp.float32) * score_scale
        masked = jnp.where(allowed, scores, -1e+30)
        row_max = lax.optimization_barrier(jnp.max(masked, axis=1, keepdims=True))
        row_sum = lax.optimization_barrier(jnp.sum(jnp.where(allowed, jnp.exp(masked - row_max), 0.0), axis=1, keepdims=True))
        log_sum = row_max + jnp.log(row_sum)
        weights = jnp.where(allowed, jnp.exp(masked - log_sum), 0.0)
        weights_low = weights.astype(jnp.bfloat16)
        out_block = jnp.dot(weights_low, value_block, preferred_element_type=jnp.float32).astype(jnp.bfloat16)
        row_dot = lax.optimization_barrier(jnp.sum(grad_block.astype(jnp.float32) * out_block.astype(jnp.float32), axis=1, keepdims=True))
        grad_weights = jnp.dot(grad_block, value_block.T, preferred_element_type=jnp.float32)
        score_grad = (weights * (grad_weights - row_dot) * score_scale).astype(jnp.bfloat16)
        query_block_grad = jnp.dot(score_grad, key_block, preferred_element_type=jnp.float32).astype(jnp.bfloat16)
        key_acc = key_acc.at[positions].add(jnp.dot(score_grad.T, query_block, preferred_element_type=jnp.float32))
        value_acc = value_acc.at[positions].add(jnp.dot(weights_low.T, grad_block, preferred_element_type=jnp.float32))
        return ((key_acc, value_acc), (out_block, query_block_grad))
    empty_grad = jnp.zeros((SEQUENCE_TOKENS, HEAD_SIZE), jnp.float32)
    sums_pair, outputs = lax.scan(block_step, (empty_grad, empty_grad), jnp.arange(NB, dtype=jnp.int32))
    return (outputs[0].reshape(SEQUENCE_TOKENS, HEAD_SIZE), outputs[1].reshape(SEQUENCE_TOKENS, HEAD_SIZE), sums_pair[0], sums_pair[1])

def reference(queries, key_vector_rows, value_vector_rows, out_grad, block_list):
    queries3 = queries.reshape(SEQUENCE_TOKENS, QUERY_HEADS, HEAD_SIZE).transpose(1, 0, 2)
    grads3 = out_grad.reshape(SEQUENCE_TOKENS, QUERY_HEADS, HEAD_SIZE).transpose(1, 0, 2)
    keys_by_head = key_vector_rows.reshape(SEQUENCE_TOKENS, KEY_VALUE_HEADS, HEAD_SIZE).transpose(1, 0, 2)
    values_by_head = value_vector_rows.reshape(SEQUENCE_TOKENS, KEY_VALUE_HEADS, HEAD_SIZE).transpose(1, 0, 2)

    def per_head(head_index):
        return head_pass(head_index, queries3, keys_by_head, values_by_head, grads3, block_list)
    attended, query_grad, key_portion, value_portion = lax.map(per_head, jnp.arange(QUERY_HEADS, dtype=jnp.int32))
    attended = attended.transpose(1, 0, 2).reshape(SEQUENCE_TOKENS, QUERY_HEADS * HEAD_SIZE)
    query_grad = query_grad.transpose(1, 0, 2).reshape(SEQUENCE_TOKENS, QUERY_HEADS * HEAD_SIZE)
    gradient_keys = key_portion.reshape(KEY_VALUE_HEADS, QUERY_HEADS // KEY_VALUE_HEADS, SEQUENCE_TOKENS, HEAD_SIZE).sum(axis=1).transpose(1, 0, 2).reshape(SEQUENCE_TOKENS, KEY_VALUE_HEADS * HEAD_SIZE).astype(jnp.bfloat16)
    gradient_values = value_portion.reshape(KEY_VALUE_HEADS, QUERY_HEADS // KEY_VALUE_HEADS, SEQUENCE_TOKENS, HEAD_SIZE).sum(axis=1).transpose(1, 0, 2).reshape(SEQUENCE_TOKENS, KEY_VALUE_HEADS * HEAD_SIZE).astype(jnp.bfloat16)
    return (attended, query_grad, gradient_keys, gradient_values)
```

```python
import math

import jax
import jax.numpy as jnp
from jax import lax
from jax.sharding import Mesh, PartitionSpec as P

KEY_VALUE_HEADS = 2
HEAD_SIZE = 128
BLOCK = 128


def body(queries, key_vector_rows, value_vector_rows, out_grad, block_list):
    ulysses_width = lax.axis_size("uly")
    cycle_size = lax.axis_size("chip") * lax.axis_size("core")
    segment_length = queries.shape[0]
    heads_dev = block_list.shape[0]
    list_len = block_list.shape[2]
    head_width = heads_dev * HEAD_SIZE
    copy_count = ulysses_width // KEY_VALUE_HEADS
    core_count = lax.axis_size("core")
    cycle_index = lax.axis_index("chip") * core_count + lax.axis_index("core")
    score_scale = 1.0 / math.sqrt(HEAD_SIZE)
    sub_length = min(segment_length, BLOCK)
    sub_count = segment_length // sub_length
    unit_len = min(segment_length, BLOCK)
    units_per_block = BLOCK // unit_len
    units_per_segment = segment_length // unit_len
    total_tokens = segment_length * ulysses_width * cycle_size
    units_total = total_tokens // unit_len
    query_slots = queries.reshape(segment_length, ulysses_width, head_width)
    grad_slots = out_grad.reshape(segment_length, ulysses_width, head_width)
    kv_local = jnp.concatenate(
        [
            key_vector_rows.reshape(segment_length, KEY_VALUE_HEADS, HEAD_SIZE),
            value_vector_rows.reshape(segment_length, KEY_VALUE_HEADS, HEAD_SIZE),
        ],
        axis=2,
    )
    kv_slots = jnp.repeat(kv_local, copy_count, axis=1)
    query_all, kv_mine, grad_all = (
        lax.all_to_all(query_slots, "uly", split_axis=1, concat_axis=0, tiled=True),
        lax.all_to_all(kv_slots, "uly", split_axis=1, concat_axis=0, tiled=True),
        lax.all_to_all(grad_slots, "uly", split_axis=1, concat_axis=0, tiled=True),
    )
    keys_chip = lax.all_gather(kv_mine[:, 0, :], "chip", axis=0, tiled=False)
    keys_all = lax.all_gather(keys_chip, "core", axis=1, tiled=False).reshape(
        cycle_size * segment_length * ulysses_width, 2 * HEAD_SIZE
    )
    item_count = heads_dev * ulysses_width * sub_count
    query_items = (
        query_all.reshape(ulysses_width, sub_count, sub_length, heads_dev, HEAD_SIZE)
        .transpose(3, 0, 1, 2, 4)
        .reshape(item_count, sub_length, HEAD_SIZE)
    )
    grad_items = (
        grad_all.reshape(ulysses_width, sub_count, sub_length, heads_dev, HEAD_SIZE)
        .transpose(3, 0, 1, 2, 4)
        .reshape(item_count, sub_length, HEAD_SIZE)
    )
    item_ids = jnp.arange(item_count, dtype=jnp.int32)
    head_ids = item_ids // (ulysses_width * sub_count)
    slot_ids = item_ids // sub_count % ulysses_width
    sub_ids = item_ids % sub_count
    segments = slot_ids * cycle_size + cycle_index
    first_pos = segments * segment_length + sub_ids * sub_length
    query_block = first_pos // BLOCK
    entries = block_list[head_ids, query_block]
    earlier = jnp.arange(list_len)[:, None] > jnp.arange(list_len)[None, :]
    repeated = jnp.any((entries[:, :, None] == entries[:, None, :]) & earlier[None, :, :], axis=2)
    offsets = jnp.arange(BLOCK, dtype=jnp.int32)
    key_pos = (entries[:, :, None] * BLOCK + offsets[None, None, :]).reshape(
        item_count, list_len * BLOCK
    )
    live_keys = jnp.repeat(jnp.logical_not(repeated), BLOCK, axis=1)
    query_pos = first_pos[:, None] + jnp.arange(sub_length, dtype=jnp.int32)[None, :]
    allowed = (key_pos[:, None, :] <= query_pos[:, :, None]) & live_keys[:, None, :]
    unit_count = list_len * units_per_block
    natural_units = (
        entries[:, :, None] * units_per_block
        + jnp.arange(units_per_block, dtype=jnp.int32)[None, None, :]
    ).reshape(item_count, unit_count)
    unit_seg = natural_units // units_per_segment
    canon_units = (
        unit_seg % cycle_size * ulysses_width + unit_seg // cycle_size
    ) * units_per_segment + natural_units % units_per_segment
    owner_of = unit_seg % cycle_size
    grad_units = (
        (owner_of % core_count * (cycle_size // core_count) + owner_of // core_count) * ulysses_width
        + unit_seg // cycle_size
    ) * units_per_segment + natural_units % units_per_segment
    keys_units = keys_all.reshape(units_total, unit_len * 2 * HEAD_SIZE)
    unit_iota = jnp.arange(units_total, dtype=jnp.int32)
    per_step = min(item_count, max(1, 512 // sub_length))
    step_count = item_count // per_step
    key_len = list_len * BLOCK

    def group_step(grad_acc, group_data):
        query_group, grad_group, fetch_group, canon_group, mask_group = group_data
        fetch_table = (fetch_group.reshape(-1)[:, None] == unit_iota[None, :]).astype(jnp.bfloat16)
        gathered = (
            jnp.dot(fetch_table, keys_units, preferred_element_type=jnp.float32)
            .astype(jnp.bfloat16)
            .reshape(per_step, key_len, 2 * HEAD_SIZE)
        )
        key_group = gathered[:, :, :HEAD_SIZE]
        value_group = gathered[:, :, HEAD_SIZE:]
        scores = (
            jnp.einsum("nqd,nkd->nqk", query_group, key_group, preferred_element_type=jnp.float32)
            * score_scale
        )
        masked = jnp.where(mask_group, scores, -1e30)
        row_max = jnp.max(masked, axis=2, keepdims=True)
        row_sum = jnp.sum(
            jnp.where(mask_group, jnp.exp(masked - row_max), 0.0), axis=2, keepdims=True
        )
        log_sum = row_max + jnp.log(row_sum)
        weights = jnp.where(mask_group, jnp.exp(masked - log_sum), 0.0)
        weights_low = weights.astype(jnp.bfloat16)
        out_group = jnp.einsum(
            "nqk,nkd->nqd", weights_low, value_group, preferred_element_type=jnp.float32
        ).astype(jnp.bfloat16)
        row_dot = jnp.sum(
            grad_group.astype(jnp.float32) * out_group.astype(jnp.float32), axis=2, keepdims=True
        )
        grad_weights = jnp.einsum(
            "nqd,nkd->nqk", grad_group, value_group, preferred_element_type=jnp.float32
        )
        score_grad = (weights * (grad_weights - row_dot) * score_scale).astype(jnp.bfloat16)
        query_group_grad = jnp.einsum(
            "nqk,nkd->nqd", score_grad, key_group, preferred_element_type=jnp.float32
        ).astype(jnp.bfloat16)
        key_portion = jnp.einsum(
            "nqk,nqd->nkd", score_grad, query_group, preferred_element_type=jnp.float32
        )
        value_portion = jnp.einsum(
            "nqk,nqd->nkd", weights_low, grad_group, preferred_element_type=jnp.float32
        )
        both_parts = jnp.concatenate([key_portion, value_portion], axis=2).reshape(
            per_step * unit_count, unit_len * 2 * HEAD_SIZE
        )
        place_table = (canon_group.reshape(-1)[:, None] == unit_iota[None, :]).astype(jnp.float32)
        grad_acc = grad_acc + jnp.dot(
            place_table.T,
            both_parts,
            preferred_element_type=jnp.float32,
            precision=lax.Precision.HIGHEST,
        )
        return (grad_acc, (out_group, query_group_grad))

    empty_grad = jnp.zeros((units_total, unit_len * 2 * HEAD_SIZE), jnp.float32)
    scan_inputs = (
        query_items.reshape(step_count, per_step, sub_length, HEAD_SIZE),
        grad_items.reshape(step_count, per_step, sub_length, HEAD_SIZE),
        canon_units.reshape(step_count, per_step, unit_count),
        grad_units.reshape(step_count, per_step, unit_count),
        allowed.reshape(step_count, per_step, sub_length, key_len),
    )
    unit_grads, item_outputs = lax.scan(group_step, empty_grad, scan_inputs)
    out_items = (
        item_outputs[0]
        .reshape(heads_dev, ulysses_width, sub_count, sub_length, HEAD_SIZE)
        .transpose(1, 2, 3, 0, 4)
        .reshape(ulysses_width * segment_length, 1, head_width)
    )
    qgrad_items = (
        item_outputs[1]
        .reshape(heads_dev, ulysses_width, sub_count, sub_length, HEAD_SIZE)
        .transpose(1, 2, 3, 0, 4)
        .reshape(ulysses_width * segment_length, 1, head_width)
    )
    attended_back, qgrad_back = (
        lax.all_to_all(out_items, "uly", split_axis=0, concat_axis=1, tiled=True),
        lax.all_to_all(qgrad_items, "uly", split_axis=0, concat_axis=1, tiled=True),
    )
    attended = attended_back.reshape(segment_length, ulysses_width * head_width)
    query_grad = qgrad_back.reshape(segment_length, ulysses_width * head_width)
    grad_split = unit_grads.reshape(
        core_count, cycle_size // core_count, ulysses_width * segment_length, 2 * HEAD_SIZE
    )
    core_index = lax.axis_index("core")
    kept = lax.dynamic_index_in_dim(grad_split, core_index, axis=0, keepdims=False)
    sent = lax.dynamic_index_in_dim(grad_split, 1 - core_index, axis=0, keepdims=False)
    received = lax.ppermute(sent, "core", [(0, 1), (1, 0)])
    owned = lax.psum_scatter(kept + received, "chip", scatter_dimension=0, tiled=True)
    result_tuple = lax.all_to_all(
        owned.reshape(ulysses_width * segment_length, 1, 2 * HEAD_SIZE),
        "uly",
        split_axis=0,
        concat_axis=1,
        tiled=True,
    )
    summed_total = result_tuple.reshape(
        segment_length, KEY_VALUE_HEADS, copy_count, 2 * HEAD_SIZE
    ).sum(axis=2)
    gradient_keys = (
        summed_total[:, :, :HEAD_SIZE]
        .reshape(segment_length, KEY_VALUE_HEADS * HEAD_SIZE)
        .astype(jnp.bfloat16)
    )
    gradient_values = (
        summed_total[:, :, HEAD_SIZE:]
        .reshape(segment_length, KEY_VALUE_HEADS * HEAD_SIZE)
        .astype(jnp.bfloat16)
    )
    return (attended, query_grad, gradient_keys, gradient_values)


def solution(mesh):
    devices = mesh.devices
    cores = 2
    fine_mesh = Mesh(
        devices.reshape(devices.shape[0], devices.shape[1] // cores, cores), ("uly", "chip", "core")
    )
    rows = P(("uly", "chip", "core"), None)
    in_specs = (rows, rows, rows, rows, P("uly", None, None))
    out_specs = (rows, rows, rows, rows)
    return jax.shard_map(body, mesh=fine_mesh, in_specs=in_specs, out_specs=out_specs, check_vma=False)
```

```python
import functools
import math

import jax
import jax.numpy as jnp
from jax import lax
from jax.experimental import pallas as pl
from jax.experimental.pallas import tpu as pltpu
from jax.sharding import PartitionSpec as P

KEY_VALUE_HEADS = 2
HEAD_SIZE = 128
BLOCK = 128


def attention_kernel(
    tab_ref, q_ref, g_ref, kv_ref, out_ref, dq_ref, dkv_ref, kvg_ref,
    *, heads_dev, slots, seg_len, list_len, units_per_block, score_scale,
):
    dkv_ref[...] = jnp.zeros(dkv_ref.shape, jnp.float32)
    n_items = heads_dev * slots
    key_len = list_len * BLOCK
    base_at = n_items
    rows_at = n_items + n_items * list_len
    lane = lax.broadcasted_iota(jnp.int32, (1, key_len), 1)
    lane_block = lane // BLOCK
    lane_offset = lane % BLOCK
    query_offset = lax.broadcasted_iota(jnp.int32, (seg_len, 1), 0)
    nt = (((1,), (1,)), ((), ()))
    tn = (((0,), (0,)), ((), ()))
    for head in range(heads_dev):
        cols = slice(head * HEAD_SIZE, (head + 1) * HEAD_SIZE)

        def item_step(slot, carry, head=head, cols=cols):
            item = head * slots + slot
            rows = pl.ds(pl.multiple_of(slot * seg_len, seg_len), seg_len)
            query_block = q_ref[rows, cols]
            grad_block = g_ref[rows, cols]
            key_pos = lane_offset
            base = jnp.zeros((1, key_len), jnp.int32)
            for j in range(list_len):
                base = jnp.where(lane_block == j, tab_ref[base_at + item * list_len + j], base)
                for u in range(units_per_block):
                    src = tab_ref[rows_at + (item * list_len + j) * units_per_block + u]
                    kvg_ref[pl.ds(j * BLOCK + u * seg_len, seg_len), :] = kv_ref[
                        pl.ds(pl.multiple_of(src, seg_len), seg_len), :
                    ]
            key_pos = base + lane_offset
            query_pos = tab_ref[item] + query_offset
            allowed = key_pos <= query_pos
            key_group = kvg_ref[:, :HEAD_SIZE]
            value_group = kvg_ref[:, HEAD_SIZE:]
            scores = (
                lax.dot_general(query_block, key_group, nt, preferred_element_type=jnp.float32)
                * score_scale
            )
            masked = jnp.where(allowed, scores, -1e30)
            row_max = jnp.max(masked, axis=1, keepdims=True)
            row_sum = jnp.sum(
                jnp.where(allowed, jnp.exp(masked - row_max), 0.0), axis=1, keepdims=True
            )
            log_sum = row_max + jnp.log(row_sum)
            weights = jnp.where(allowed, jnp.exp(masked - log_sum), 0.0)
            weights_low = weights.astype(jnp.bfloat16)
            out_block = jnp.dot(
                weights_low, value_group, preferred_element_type=jnp.float32
            ).astype(jnp.bfloat16)
            out_ref[rows, cols] = out_block
            row_dot = jnp.sum(
                grad_block.astype(jnp.float32) * out_block.astype(jnp.float32),
                axis=1,
                keepdims=True,
            )
            grad_weights = lax.dot_general(
                grad_block, value_group, nt, preferred_element_type=jnp.float32
            )
            score_grad = (weights * (grad_weights - row_dot) * score_scale).astype(jnp.bfloat16)
            dq_ref[rows, cols] = jnp.dot(
                score_grad, key_group, preferred_element_type=jnp.float32
            ).astype(jnp.bfloat16)
            key_part = lax.dot_general(score_grad, query_block, tn, preferred_element_type=jnp.float32)
            value_part = lax.dot_general(weights_low, grad_block, tn, preferred_element_type=jnp.float32)
            for j in range(list_len):
                for u in range(units_per_block):
                    dst = tab_ref[rows_at + (item * list_len + j) * units_per_block + u]
                    dst_rows = pl.ds(pl.multiple_of(dst, seg_len), seg_len)
                    lo = j * BLOCK + u * seg_len
                    dkv_ref[dst_rows, :HEAD_SIZE] += key_part[lo : lo + seg_len]
                    dkv_ref[dst_rows, HEAD_SIZE:] += value_part[lo : lo + seg_len]
            return carry

        lax.fori_loop(0, slots, item_step, 0)


def body(queries, key_vector_rows, value_vector_rows, out_grad, block_list):
    ulysses_width = lax.axis_size("uly")
    cycle_size = lax.axis_size("blk")
    segment_length = queries.shape[0]
    heads_dev = block_list.shape[0]
    list_len = block_list.shape[2]
    head_width = heads_dev * HEAD_SIZE
    copy_count = ulysses_width // KEY_VALUE_HEADS
    cycle_index = lax.axis_index("blk")
    score_scale = 1.0 / math.sqrt(HEAD_SIZE)
    sub_length = min(segment_length, BLOCK)
    sub_count = segment_length // sub_length
    unit_len = min(segment_length, BLOCK)
    units_per_block = BLOCK // unit_len
    units_per_segment = segment_length // unit_len
    total_tokens = segment_length * ulysses_width * cycle_size
    units_total = total_tokens // unit_len
    query_slots = queries.reshape(segment_length, ulysses_width, head_width)
    grad_slots = out_grad.reshape(segment_length, ulysses_width, head_width)
    kv_local = jnp.concatenate(
        [
            key_vector_rows.reshape(segment_length, KEY_VALUE_HEADS, HEAD_SIZE),
            value_vector_rows.reshape(segment_length, KEY_VALUE_HEADS, HEAD_SIZE),
        ],
        axis=2,
    )
    kv_slots = jnp.repeat(kv_local, copy_count, axis=1)
    query_all, kv_mine, grad_all = (
        lax.all_to_all(query_slots, "uly", split_axis=1, concat_axis=0, tiled=True),
        lax.all_to_all(kv_slots, "uly", split_axis=1, concat_axis=0, tiled=True),
        lax.all_to_all(grad_slots, "uly", split_axis=1, concat_axis=0, tiled=True),
    )
    keys_all = lax.all_gather(kv_mine[:, 0, :], "blk", axis=0, tiled=True)
    item_count = heads_dev * ulysses_width
    item_ids = jnp.arange(item_count, dtype=jnp.int32)
    head_ids = item_ids // ulysses_width
    slot_ids = item_ids % ulysses_width
    first_pos = (slot_ids * cycle_size + cycle_index) * segment_length
    entries = block_list[head_ids, first_pos // BLOCK]
    earlier = jnp.arange(list_len)[:, None] > jnp.arange(list_len)[None, :]
    repeated = jnp.any((entries[:, :, None] == entries[:, None, :]) & earlier[None, :, :], axis=2)
    key_base = jnp.where(repeated, 1 << 30, entries * BLOCK)
    units_per_block = BLOCK // segment_length
    natural_segs = (
        entries[:, :, None] * units_per_block
        + jnp.arange(units_per_block, dtype=jnp.int32)[None, None, :]
    )
    canon_rows = (
        natural_segs % cycle_size * ulysses_width + natural_segs // cycle_size
    ) * segment_length
    table = jnp.concatenate(
        [first_pos.reshape(-1), key_base.reshape(-1), canon_rows.reshape(-1)]
    ).astype(jnp.int32)
    q_rows = query_all.reshape(ulysses_width * segment_length, head_width)
    g_rows = grad_all.reshape(ulysses_width * segment_length, head_width)
    kernel = functools.partial(
        attention_kernel,
        heads_dev=heads_dev,
        slots=ulysses_width,
        seg_len=segment_length,
        list_len=list_len,
        units_per_block=units_per_block,
        score_scale=score_scale,
    )
    out_rows, qgrad_rows, kv_grad_all = pl.pallas_call(
        kernel,
        out_shape=(
            jax.ShapeDtypeStruct(q_rows.shape, jnp.bfloat16),
            jax.ShapeDtypeStruct(q_rows.shape, jnp.bfloat16),
            jax.ShapeDtypeStruct(keys_all.shape, jnp.float32),
        ),
        in_specs=[
            pl.BlockSpec(memory_space=pltpu.SMEM),
            pl.BlockSpec(memory_space=pltpu.VMEM),
            pl.BlockSpec(memory_space=pltpu.VMEM),
            pl.BlockSpec(memory_space=pltpu.VMEM),
        ],
        out_specs=(
            pl.BlockSpec(memory_space=pltpu.VMEM),
            pl.BlockSpec(memory_space=pltpu.VMEM),
            pl.BlockSpec(memory_space=pltpu.VMEM),
        ),
        scratch_shapes=[pltpu.VMEM((list_len * BLOCK, 2 * HEAD_SIZE), jnp.bfloat16)],
        compiler_params=pltpu.CompilerParams(vmem_limit_bytes=48 * 1024 * 1024),
    )(table, q_rows, g_rows, keys_all)
    out_items = out_rows.reshape(ulysses_width * segment_length, 1, head_width)
    qgrad_items = qgrad_rows.reshape(ulysses_width * segment_length, 1, head_width)
    attended_back, qgrad_back = (
        lax.all_to_all(out_items, "uly", split_axis=0, concat_axis=1, tiled=True),
        lax.all_to_all(qgrad_items, "uly", split_axis=0, concat_axis=1, tiled=True),
    )
    attended = attended_back.reshape(segment_length, ulysses_width * head_width)
    query_grad = qgrad_back.reshape(segment_length, ulysses_width * head_width)
    owned = lax.psum_scatter(kv_grad_all, "blk", scatter_dimension=0, tiled=True)
    result_tuple = lax.all_to_all(
        owned.reshape(ulysses_width * segment_length, 1, 2 * HEAD_SIZE),
        "uly",
        split_axis=0,
        concat_axis=1,
        tiled=True,
    )
    summed_total = result_tuple.reshape(
        segment_length, KEY_VALUE_HEADS, copy_count, 2 * HEAD_SIZE
    ).sum(axis=2)
    gradient_keys = (
        summed_total[:, :, :HEAD_SIZE]
        .reshape(segment_length, KEY_VALUE_HEADS * HEAD_SIZE)
        .astype(jnp.bfloat16)
    )
    gradient_values = (
        summed_total[:, :, HEAD_SIZE:]
        .reshape(segment_length, KEY_VALUE_HEADS * HEAD_SIZE)
        .astype(jnp.bfloat16)
    )
    return (attended, query_grad, gradient_keys, gradient_values)


def solution(mesh):
    in_specs = (
        P(("uly", "blk"), None),
        P(("uly", "blk"), None),
        P(("uly", "blk"), None),
        P(("uly", "blk"), None),
        P("uly", None, None),
    )
    out_specs = (
        P(("uly", "blk"), None),
        P(("uly", "blk"), None),
        P(("uly", "blk"), None),
        P(("uly", "blk"), None),
    )
    return jax.shard_map(body, mesh=mesh, in_specs=in_specs, out_specs=out_specs, check_vma=False)
```

```python
import functools
import math

import jax
import jax.numpy as jnp
from jax import lax
from jax.experimental import pallas as pl
from jax.experimental.pallas import tpu as pltpu
from jax.sharding import Mesh, PartitionSpec as P

KEY_VALUE_HEADS = 2
HEAD_SIZE = 128
BLOCK = 128


def attention_kernel(
    tab_ref, q_ref, g_ref, kv_ref, out_ref, dq_ref, dkv_ref, kvg_ref,
    *, heads_dev, slots, seg_len, list_len, units_per_block, score_scale,
):
    dkv_ref[...] = jnp.zeros(dkv_ref.shape, jnp.float32)
    n_items = heads_dev * slots
    key_len = list_len * BLOCK
    base_at = n_items
    rows_at = n_items + n_items * list_len
    lane = lax.broadcasted_iota(jnp.int32, (1, key_len), 1)
    lane_block = lane // BLOCK
    lane_offset = lane % BLOCK
    query_offset = lax.broadcasted_iota(jnp.int32, (seg_len, 1), 0)
    nt = (((1,), (1,)), ((), ()))
    tn = (((0,), (0,)), ((), ()))
    for head in range(heads_dev):
        cols = slice(head * HEAD_SIZE, (head + 1) * HEAD_SIZE)

        def item_step(slot, carry, head=head, cols=cols):
            item = head * slots + slot
            rows = pl.ds(pl.multiple_of(slot * seg_len, seg_len), seg_len)
            query_block = q_ref[rows, cols]
            grad_block = g_ref[rows, cols]
            key_pos = lane_offset
            base = jnp.zeros((1, key_len), jnp.int32)
            for j in range(list_len):
                base = jnp.where(lane_block == j, tab_ref[base_at + item * list_len + j], base)
                for u in range(units_per_block):
                    src = tab_ref[rows_at + (item * list_len + j) * units_per_block + u]
                    kvg_ref[pl.ds(j * BLOCK + u * seg_len, seg_len), :] = kv_ref[
                        pl.ds(pl.multiple_of(src, seg_len), seg_len), :
                    ]
            key_pos = base + lane_offset
            query_pos = tab_ref[item] + query_offset
            allowed = key_pos <= query_pos
            key_group = kvg_ref[:, :HEAD_SIZE]
            value_group = kvg_ref[:, HEAD_SIZE:]
            scores = (
                lax.dot_general(query_block, key_group, nt, preferred_element_type=jnp.float32)
                * score_scale
            )
            masked = jnp.where(allowed, scores, -1e30)
            row_max = jnp.max(masked, axis=1, keepdims=True)
            row_sum = jnp.sum(
                jnp.where(allowed, jnp.exp(masked - row_max), 0.0), axis=1, keepdims=True
            )
            log_sum = row_max + jnp.log(row_sum)
            weights = jnp.where(allowed, jnp.exp(masked - log_sum), 0.0)
            weights_low = weights.astype(jnp.bfloat16)
            out_block = jnp.dot(
                weights_low, value_group, preferred_element_type=jnp.float32
            ).astype(jnp.bfloat16)
            out_ref[rows, cols] = out_block
            row_dot = jnp.sum(
                grad_block.astype(jnp.float32) * out_block.astype(jnp.float32),
                axis=1,
                keepdims=True,
            )
            grad_weights = lax.dot_general(
                grad_block, value_group, nt, preferred_element_type=jnp.float32
            )
            score_grad = (weights * (grad_weights - row_dot) * score_scale).astype(jnp.bfloat16)
            dq_ref[rows, cols] = jnp.dot(
                score_grad, key_group, preferred_element_type=jnp.float32
            ).astype(jnp.bfloat16)
            key_part = lax.dot_general(score_grad, query_block, tn, preferred_element_type=jnp.float32)
            value_part = lax.dot_general(weights_low, grad_block, tn, preferred_element_type=jnp.float32)
            for j in range(list_len):
                for u in range(units_per_block):
                    dst = tab_ref[rows_at + (item * list_len + j) * units_per_block + u]
                    dst_rows = pl.ds(pl.multiple_of(dst, seg_len), seg_len)
                    lo = j * BLOCK + u * seg_len
                    dkv_ref[dst_rows, :HEAD_SIZE] += key_part[lo : lo + seg_len]
                    dkv_ref[dst_rows, HEAD_SIZE:] += value_part[lo : lo + seg_len]
            return carry

        lax.fori_loop(0, slots, item_step, 0)


def body(queries, key_vector_rows, value_vector_rows, out_grad, block_list):
    group_count = lax.axis_size("xh")
    row_count = lax.axis_size("y")
    ulysses_width = group_count * row_count
    cycle_size = lax.axis_size("blk")
    segment_length = queries.shape[0]
    heads_dev = block_list.shape[0]
    list_len = block_list.shape[2]
    head_width = heads_dev * HEAD_SIZE
    copy_count = ulysses_width // KEY_VALUE_HEADS
    cycle_index = lax.axis_index("blk")
    score_scale = 1.0 / math.sqrt(HEAD_SIZE)
    sub_length = min(segment_length, BLOCK)
    sub_count = segment_length // sub_length
    unit_len = min(segment_length, BLOCK)
    units_per_block = BLOCK // unit_len
    units_per_segment = segment_length // unit_len
    total_tokens = segment_length * ulysses_width * cycle_size
    units_total = total_tokens // unit_len
    query_slots = queries.reshape(segment_length, ulysses_width, head_width)
    grad_slots = out_grad.reshape(segment_length, ulysses_width, head_width)
    kv_local = jnp.concatenate(
        [
            key_vector_rows.reshape(segment_length, KEY_VALUE_HEADS, HEAD_SIZE),
            value_vector_rows.reshape(segment_length, KEY_VALUE_HEADS, HEAD_SIZE),
        ],
        axis=2,
    )
    kv_by_group = kv_local.transpose(1, 0, 2)
    kv_pair = lax.all_to_all(kv_by_group, "xh", split_axis=0, concat_axis=0, tiled=True)
    keys_all = lax.all_gather(
        kv_pair.reshape(group_count * segment_length, 2 * HEAD_SIZE),
        ("y", "blk"),
        axis=0,
        tiled=True,
    )
    query_all, grad_all = (
        lax.all_to_all(query_slots, ("xh", "y"), split_axis=1, concat_axis=0, tiled=True),
        lax.all_to_all(grad_slots, ("xh", "y"), split_axis=1, concat_axis=0, tiled=True),
    )
    item_count = heads_dev * ulysses_width
    item_ids = jnp.arange(item_count, dtype=jnp.int32)
    head_ids = item_ids // ulysses_width
    slot_ids = item_ids % ulysses_width
    first_pos = (slot_ids * cycle_size + cycle_index) * segment_length
    entries = block_list[head_ids, first_pos // BLOCK]
    earlier = jnp.arange(list_len)[:, None] > jnp.arange(list_len)[None, :]
    repeated = jnp.any((entries[:, :, None] == entries[:, None, :]) & earlier[None, :, :], axis=2)
    key_base = jnp.where(repeated, 1 << 30, entries * BLOCK)
    units_per_block = BLOCK // segment_length
    natural_segs = (
        entries[:, :, None] * units_per_block
        + jnp.arange(units_per_block, dtype=jnp.int32)[None, None, :]
    )
    seg_slot = natural_segs // cycle_size
    canon_rows = (
        (seg_slot % row_count * cycle_size + natural_segs % cycle_size) * group_count
        + seg_slot // row_count
    ) * segment_length
    table = jnp.concatenate(
        [first_pos.reshape(-1), key_base.reshape(-1), canon_rows.reshape(-1)]
    ).astype(jnp.int32)
    q_rows = query_all.reshape(ulysses_width * segment_length, head_width)
    g_rows = grad_all.reshape(ulysses_width * segment_length, head_width)
    kernel = functools.partial(
        attention_kernel,
        heads_dev=heads_dev,
        slots=ulysses_width,
        seg_len=segment_length,
        list_len=list_len,
        units_per_block=units_per_block,
        score_scale=score_scale,
    )
    out_rows, qgrad_rows, kv_grad_all = pl.pallas_call(
        kernel,
        out_shape=(
            jax.ShapeDtypeStruct(q_rows.shape, jnp.bfloat16),
            jax.ShapeDtypeStruct(q_rows.shape, jnp.bfloat16),
            jax.ShapeDtypeStruct(keys_all.shape, jnp.float32),
        ),
        in_specs=[
            pl.BlockSpec(memory_space=pltpu.SMEM),
            pl.BlockSpec(memory_space=pltpu.VMEM),
            pl.BlockSpec(memory_space=pltpu.VMEM),
            pl.BlockSpec(memory_space=pltpu.VMEM),
        ],
        out_specs=(
            pl.BlockSpec(memory_space=pltpu.VMEM),
            pl.BlockSpec(memory_space=pltpu.VMEM),
            pl.BlockSpec(memory_space=pltpu.VMEM),
        ),
        scratch_shapes=[pltpu.VMEM((list_len * BLOCK, 2 * HEAD_SIZE), jnp.bfloat16)],
        compiler_params=pltpu.CompilerParams(vmem_limit_bytes=48 * 1024 * 1024),
    )(table, q_rows, g_rows, keys_all)
    out_items = out_rows.reshape(ulysses_width * segment_length, 1, head_width)
    qgrad_items = qgrad_rows.reshape(ulysses_width * segment_length, 1, head_width)
    attended_back, qgrad_back = (
        lax.all_to_all(out_items, ("xh", "y"), split_axis=0, concat_axis=1, tiled=True),
        lax.all_to_all(qgrad_items, ("xh", "y"), split_axis=0, concat_axis=1, tiled=True),
    )
    attended = attended_back.reshape(segment_length, ulysses_width * head_width)
    query_grad = qgrad_back.reshape(segment_length, ulysses_width * head_width)
    owned = lax.psum_scatter(kv_grad_all, ("y", "blk"), scatter_dimension=0, tiled=True)
    by_group = lax.all_to_all(
        owned.reshape(group_count, segment_length, 2 * HEAD_SIZE),
        "xh",
        split_axis=0,
        concat_axis=0,
        tiled=True,
    ).transpose(1, 0, 2)
    gradient_keys = (
        by_group[:, :, :HEAD_SIZE]
        .reshape(segment_length, group_count * HEAD_SIZE)
        .astype(jnp.bfloat16)
    )
    gradient_values = (
        by_group[:, :, HEAD_SIZE:]
        .reshape(segment_length, group_count * HEAD_SIZE)
        .astype(jnp.bfloat16)
    )
    return (attended, query_grad, gradient_keys, gradient_values)


def solution(mesh):
    devices = mesh.devices
    fine_mesh = Mesh(
        devices.reshape(KEY_VALUE_HEADS, devices.shape[0] // KEY_VALUE_HEADS, devices.shape[1]),
        ("xh", "y", "blk"),
    )
    rows = P(("xh", "y", "blk"), None)
    in_specs = (rows, rows, rows, rows, P(("xh", "y"), None, None))
    out_specs = (rows, rows, rows, rows)
    return jax.shard_map(body, mesh=fine_mesh, in_specs=in_specs, out_specs=out_specs, check_vma=False)
```

```python
import functools
import math

import jax
import jax.numpy as jnp
from jax import lax
from jax.experimental import pallas as pl
from jax.experimental.pallas import tpu as pltpu
from jax.sharding import Mesh, PartitionSpec as P

KEY_VALUE_HEADS = 2
HEAD_SIZE = 128
BLOCK = 128


def attention_kernel(
    tab_ref, q_ref, g_ref, kv_ref, out_ref, dq_ref, dkv_ref, kvg_ref,
    *, heads_dev, slots, seg_len, list_len, units_per_block, score_scale,
):
    dkv_ref[...] = jnp.zeros(dkv_ref.shape, jnp.float32)
    n_items = heads_dev * slots
    key_len = list_len * BLOCK
    base_at = n_items
    rows_at = n_items + n_items * list_len
    grad_at = rows_at + n_items * list_len * units_per_block
    plane_rows = dkv_ref.shape[1]
    lane = lax.broadcasted_iota(jnp.int32, (1, key_len), 1)
    lane_block = lane // BLOCK
    lane_offset = lane % BLOCK
    query_offset = lax.broadcasted_iota(jnp.int32, (seg_len, 1), 0)
    nt = (((1,), (1,)), ((), ()))
    tn = (((0,), (0,)), ((), ()))
    for head in range(heads_dev):
        cols = slice(head * HEAD_SIZE, (head + 1) * HEAD_SIZE)

        def item_step(slot, carry, head=head, cols=cols):
            item = head * slots + slot
            rows = pl.ds(pl.multiple_of(slot * seg_len, seg_len), seg_len)
            query_block = q_ref[rows, cols]
            grad_block = g_ref[rows, cols]
            key_pos = lane_offset
            base = jnp.zeros((1, key_len), jnp.int32)
            for j in range(list_len):
                base = jnp.where(lane_block == j, tab_ref[base_at + item * list_len + j], base)
                for u in range(units_per_block):
                    src = tab_ref[rows_at + (item * list_len + j) * units_per_block + u]
                    kvg_ref[pl.ds(j * BLOCK + u * seg_len, seg_len), :] = kv_ref[
                        pl.ds(pl.multiple_of(src, seg_len), seg_len), :
                    ]
            key_pos = base + lane_offset
            query_pos = tab_ref[item] + query_offset
            allowed = key_pos <= query_pos
            key_group = kvg_ref[:, :HEAD_SIZE]
            value_group = kvg_ref[:, HEAD_SIZE:]
            scores = (
                lax.dot_general(query_block, key_group, nt, preferred_element_type=jnp.float32)
                * score_scale
            )
            masked = jnp.where(allowed, scores, -1e30)
            row_max = jnp.max(masked, axis=1, keepdims=True)
            row_sum = jnp.sum(
                jnp.where(allowed, jnp.exp(masked - row_max), 0.0), axis=1, keepdims=True
            )
            log_sum = row_max + jnp.log(row_sum)
            weights = jnp.where(allowed, jnp.exp(masked - log_sum), 0.0)
            weights_low = weights.astype(jnp.bfloat16)
            out_block = jnp.dot(
                weights_low, value_group, preferred_element_type=jnp.float32
            ).astype(jnp.bfloat16)
            out_ref[rows, cols] = out_block
            row_dot = jnp.sum(
                grad_block.astype(jnp.float32) * out_block.astype(jnp.float32),
                axis=1,
                keepdims=True,
            )
            grad_weights = lax.dot_general(
                grad_block, value_group, nt, preferred_element_type=jnp.float32
            )
            score_grad = (weights * (grad_weights - row_dot) * score_scale).astype(jnp.bfloat16)
            dq_ref[rows, cols] = jnp.dot(
                score_grad, key_group, preferred_element_type=jnp.float32
            ).astype(jnp.bfloat16)
            key_part = lax.dot_general(score_grad, query_block, tn, preferred_element_type=jnp.float32)
            value_part = lax.dot_general(weights_low, grad_block, tn, preferred_element_type=jnp.float32)
            for j in range(list_len):
                for u in range(units_per_block):
                    dst = tab_ref[grad_at + (item * list_len + j) * units_per_block + u]
                    plane = dst // plane_rows
                    dst_rows = pl.ds(pl.multiple_of(dst % plane_rows, seg_len), seg_len)
                    lo = j * BLOCK + u * seg_len
                    dkv_ref[plane, dst_rows, :HEAD_SIZE] += key_part[lo : lo + seg_len]
                    dkv_ref[plane, dst_rows, HEAD_SIZE:] += value_part[lo : lo + seg_len]
            return carry

        lax.fori_loop(0, slots, item_step, 0)


def body(queries, key_vector_rows, value_vector_rows, out_grad, block_list):
    ulysses_width = lax.axis_size("uly")
    core_count = lax.axis_size("core")
    chip_count = lax.axis_size("chip")
    cycle_size = chip_count * core_count
    segment_length = queries.shape[0]
    heads_dev = block_list.shape[0]
    list_len = block_list.shape[2]
    head_width = heads_dev * HEAD_SIZE
    copy_count = ulysses_width // KEY_VALUE_HEADS
    core_index = lax.axis_index("core")
    cycle_index = lax.axis_index("chip") * core_count + core_index
    score_scale = 1.0 / math.sqrt(HEAD_SIZE)
    sub_length = min(segment_length, BLOCK)
    sub_count = segment_length // sub_length
    unit_len = min(segment_length, BLOCK)
    units_per_block = BLOCK // unit_len
    units_per_segment = segment_length // unit_len
    total_tokens = segment_length * ulysses_width * cycle_size
    units_total = total_tokens // unit_len
    query_slots = queries.reshape(segment_length, ulysses_width, head_width)
    grad_slots = out_grad.reshape(segment_length, ulysses_width, head_width)
    kv_local = jnp.concatenate(
        [
            key_vector_rows.reshape(segment_length, KEY_VALUE_HEADS, HEAD_SIZE),
            value_vector_rows.reshape(segment_length, KEY_VALUE_HEADS, HEAD_SIZE),
        ],
        axis=2,
    )
    kv_slots = jnp.repeat(kv_local, copy_count, axis=1)
    query_all, kv_mine, grad_all = (
        lax.all_to_all(query_slots, "uly", split_axis=1, concat_axis=0, tiled=True),
        lax.all_to_all(kv_slots, "uly", split_axis=1, concat_axis=0, tiled=True),
        lax.all_to_all(grad_slots, "uly", split_axis=1, concat_axis=0, tiled=True),
    )
    keys_all = lax.all_gather(kv_mine[:, 0, :], ("chip", "core"), axis=0, tiled=True)
    item_count = heads_dev * ulysses_width
    item_ids = jnp.arange(item_count, dtype=jnp.int32)
    head_ids = item_ids // ulysses_width
    slot_ids = item_ids % ulysses_width
    first_pos = (slot_ids * cycle_size + cycle_index) * segment_length
    entries = block_list[head_ids, first_pos // BLOCK]
    earlier = jnp.arange(list_len)[:, None] > jnp.arange(list_len)[None, :]
    repeated = jnp.any((entries[:, :, None] == entries[:, None, :]) & earlier[None, :, :], axis=2)
    key_base = jnp.where(repeated, 1 << 30, entries * BLOCK)
    units_per_block = BLOCK // segment_length
    natural_segs = (
        entries[:, :, None] * units_per_block
        + jnp.arange(units_per_block, dtype=jnp.int32)[None, None, :]
    )
    canon_rows = (
        natural_segs % cycle_size * ulysses_width + natural_segs // cycle_size
    ) * segment_length
    seg_owner = natural_segs % cycle_size
    grad_rows = (
        (
            (seg_owner % core_count - core_index) % core_count * chip_count
            + seg_owner // core_count
        )
        * ulysses_width
        + natural_segs // cycle_size
    ) * segment_length
    table = jnp.concatenate(
        [
            first_pos.reshape(-1),
            key_base.reshape(-1),
            canon_rows.reshape(-1),
            grad_rows.reshape(-1),
        ]
    ).astype(jnp.int32)
    q_rows = query_all.reshape(ulysses_width * segment_length, head_width)
    g_rows = grad_all.reshape(ulysses_width * segment_length, head_width)
    kernel = functools.partial(
        attention_kernel,
        heads_dev=heads_dev,
        slots=ulysses_width,
        seg_len=segment_length,
        list_len=list_len,
        units_per_block=units_per_block,
        score_scale=score_scale,
    )
    out_rows, qgrad_rows, kv_grad_all = pl.pallas_call(
        kernel,
        out_shape=(
            jax.ShapeDtypeStruct(q_rows.shape, jnp.bfloat16),
            jax.ShapeDtypeStruct(q_rows.shape, jnp.bfloat16),
            jax.ShapeDtypeStruct(
                (core_count, keys_all.shape[0] // core_count, keys_all.shape[1]), jnp.float32
            ),
        ),
        in_specs=[
            pl.BlockSpec(memory_space=pltpu.SMEM),
            pl.BlockSpec(memory_space=pltpu.VMEM),
            pl.BlockSpec(memory_space=pltpu.VMEM),
            pl.BlockSpec(memory_space=pltpu.VMEM),
        ],
        out_specs=(
            pl.BlockSpec(memory_space=pltpu.VMEM),
            pl.BlockSpec(memory_space=pltpu.VMEM),
            pl.BlockSpec(memory_space=pltpu.VMEM),
        ),
        scratch_shapes=[pltpu.VMEM((list_len * BLOCK, 2 * HEAD_SIZE), jnp.bfloat16)],
        compiler_params=pltpu.CompilerParams(vmem_limit_bytes=48 * 1024 * 1024),
    )(table, q_rows, g_rows, keys_all)
    out_items = out_rows.reshape(ulysses_width * segment_length, 1, head_width)
    qgrad_items = qgrad_rows.reshape(ulysses_width * segment_length, 1, head_width)
    attended_back, qgrad_back = (
        lax.all_to_all(out_items, "uly", split_axis=0, concat_axis=1, tiled=True),
        lax.all_to_all(qgrad_items, "uly", split_axis=0, concat_axis=1, tiled=True),
    )
    attended = attended_back.reshape(segment_length, ulysses_width * head_width)
    query_grad = qgrad_back.reshape(segment_length, ulysses_width * head_width)
    received = lax.ppermute(kv_grad_all[1], "core", [(0, 1), (1, 0)])
    chip_part = (kv_grad_all[0] + received).reshape(
        chip_count, ulysses_width * segment_length, 2 * HEAD_SIZE
    )
    owned = lax.psum_scatter(chip_part, "chip", scatter_dimension=0, tiled=True)
    result_tuple = lax.all_to_all(
        owned.reshape(ulysses_width * segment_length, 1, 2 * HEAD_SIZE),
        "uly",
        split_axis=0,
        concat_axis=1,
        tiled=True,
    )
    summed_total = result_tuple.reshape(
        segment_length, KEY_VALUE_HEADS, copy_count, 2 * HEAD_SIZE
    ).sum(axis=2)
    gradient_keys = (
        summed_total[:, :, :HEAD_SIZE]
        .reshape(segment_length, KEY_VALUE_HEADS * HEAD_SIZE)
        .astype(jnp.bfloat16)
    )
    gradient_values = (
        summed_total[:, :, HEAD_SIZE:]
        .reshape(segment_length, KEY_VALUE_HEADS * HEAD_SIZE)
        .astype(jnp.bfloat16)
    )
    return (attended, query_grad, gradient_keys, gradient_values)


def solution(mesh):
    devices = mesh.devices
    cores = 2
    fine_mesh = Mesh(
        devices.reshape(devices.shape[0], devices.shape[1] // cores, cores), ("uly", "chip", "core")
    )
    rows = P(("uly", "chip", "core"), None)
    in_specs = (rows, rows, rows, rows, P("uly", None, None))
    out_specs = (rows, rows, rows, rows)
    return jax.shard_map(body, mesh=fine_mesh, in_specs=in_specs, out_specs=out_specs, check_vma=False)
```

```python
import functools
import math

import jax
import jax.numpy as jnp
from jax import lax
from jax.experimental import pallas as pl
from jax.experimental.pallas import tpu as pltpu
from jax.sharding import Mesh, PartitionSpec as P

KEY_VALUE_HEADS = 2
HEAD_SIZE = 128
BLOCK = 128


def attention_kernel(
    *refs, heads_dev, slots, first_slot, slot_count, carry_low, seg_len, list_len,
    units_per_block, score_scale,
):
    if carry_low:
        tab_ref, q_ref, g_ref, kv_ref, low_in_ref, out_ref, dq_ref, low_ref, kvg_ref = refs
        high_ref = None
        low_ref[...] = low_in_ref[...]
    else:
        tab_ref, q_ref, g_ref, kv_ref, out_ref, dq_ref, low_ref, high_ref, kvg_ref = refs
        low_ref[...] = jnp.zeros(low_ref.shape, jnp.float32)
        high_ref[...] = jnp.zeros(high_ref.shape, jnp.float32)
    n_items = heads_dev * slots
    key_len = list_len * BLOCK
    base_at = n_items
    rows_at = n_items + n_items * list_len
    grad_at = rows_at + n_items * list_len * units_per_block
    plane_rows = low_ref.shape[1]
    half_rows = low_ref.shape[0] * plane_rows
    lane = lax.broadcasted_iota(jnp.int32, (1, key_len), 1)
    lane_block = lane // BLOCK
    lane_offset = lane % BLOCK
    query_offset = lax.broadcasted_iota(jnp.int32, (seg_len, 1), 0)
    nt = (((1,), (1,)), ((), ()))
    tn = (((0,), (0,)), ((), ()))
    for head in range(heads_dev):
        cols = slice(head * HEAD_SIZE, (head + 1) * HEAD_SIZE)

        def item_step(step, carry, head=head, cols=cols):
            slot = first_slot + step
            item = head * slots + slot
            rows = pl.ds(pl.multiple_of(slot * seg_len, seg_len), seg_len)
            out_rows = pl.ds(pl.multiple_of(step * seg_len, seg_len), seg_len)
            query_block = q_ref[rows, cols]
            grad_block = g_ref[rows, cols]
            key_pos = lane_offset
            base = jnp.zeros((1, key_len), jnp.int32)
            for j in range(list_len):
                base = jnp.where(lane_block == j, tab_ref[base_at + item * list_len + j], base)
                for u in range(units_per_block):
                    src = tab_ref[rows_at + (item * list_len + j) * units_per_block + u]
                    kvg_ref[pl.ds(j * BLOCK + u * seg_len, seg_len), :] = kv_ref[
                        pl.ds(pl.multiple_of(src, seg_len), seg_len), :
                    ]
            key_pos = base + lane_offset
            query_pos = tab_ref[item] + query_offset
            allowed = key_pos <= query_pos
            key_group = kvg_ref[:, :HEAD_SIZE]
            value_group = kvg_ref[:, HEAD_SIZE:]
            scores = (
                lax.dot_general(query_block, key_group, nt, preferred_element_type=jnp.float32)
                * score_scale
            )
            masked = jnp.where(allowed, scores, -1e30)
            row_max = jnp.max(masked, axis=1, keepdims=True)
            row_sum = jnp.sum(
                jnp.where(allowed, jnp.exp(masked - row_max), 0.0), axis=1, keepdims=True
            )
            log_sum = row_max + jnp.log(row_sum)
            weights = jnp.where(allowed, jnp.exp(masked - log_sum), 0.0)
            weights_low = weights.astype(jnp.bfloat16)
            out_block = jnp.dot(
                weights_low, value_group, preferred_element_type=jnp.float32
            ).astype(jnp.bfloat16)
            out_ref[out_rows, cols] = out_block
            row_dot = jnp.sum(
                grad_block.astype(jnp.float32) * out_block.astype(jnp.float32),
                axis=1,
                keepdims=True,
            )
            grad_weights = lax.dot_general(
                grad_block, value_group, nt, preferred_element_type=jnp.float32
            )
            score_grad = (weights * (grad_weights - row_dot) * score_scale).astype(jnp.bfloat16)
            dq_ref[out_rows, cols] = jnp.dot(
                score_grad, key_group, preferred_element_type=jnp.float32
            ).astype(jnp.bfloat16)
            key_part = lax.dot_general(score_grad, query_block, tn, preferred_element_type=jnp.float32)
            value_part = lax.dot_general(weights_low, grad_block, tn, preferred_element_type=jnp.float32)
            for j in range(list_len):
                for u in range(units_per_block):
                    dst = tab_ref[grad_at + (item * list_len + j) * units_per_block + u]
                    half = dst // half_rows
                    plane = dst // plane_rows % 2
                    dst_rows = pl.ds(pl.multiple_of(dst % plane_rows, seg_len), seg_len)
                    lo = j * BLOCK + u * seg_len
                    key_rows = key_part[lo : lo + seg_len]
                    value_rows = value_part[lo : lo + seg_len]

                    @pl.when(half == 0)
                    def _(plane=plane, dst_rows=dst_rows, key_rows=key_rows, value_rows=value_rows):
                        low_ref[plane, dst_rows, :HEAD_SIZE] += key_rows
                        low_ref[plane, dst_rows, HEAD_SIZE:] += value_rows

                    if high_ref is not None:

                        @pl.when(half != 0)
                        def _(plane=plane, dst_rows=dst_rows, key_rows=key_rows, value_rows=value_rows):
                            high_ref[plane, dst_rows, :HEAD_SIZE] += key_rows
                            high_ref[plane, dst_rows, HEAD_SIZE:] += value_rows
            return carry

        lax.fori_loop(0, slot_count, item_step, 0)


def body(queries, key_vector_rows, value_vector_rows, out_grad, block_list):
    ulysses_width = lax.axis_size("uly")
    core_count = lax.axis_size("core")
    chip_count = lax.axis_size("chip")
    cycle_size = chip_count * core_count
    segment_length = queries.shape[0]
    heads_dev = block_list.shape[0]
    list_len = block_list.shape[2]
    head_width = heads_dev * HEAD_SIZE
    copy_count = ulysses_width // KEY_VALUE_HEADS
    core_index = lax.axis_index("core")
    cycle_index = lax.axis_index("chip") * core_count + core_index
    score_scale = 1.0 / math.sqrt(HEAD_SIZE)
    sub_length = min(segment_length, BLOCK)
    sub_count = segment_length // sub_length
    unit_len = min(segment_length, BLOCK)
    units_per_block = BLOCK // unit_len
    units_per_segment = segment_length // unit_len
    total_tokens = segment_length * ulysses_width * cycle_size
    units_total = total_tokens // unit_len
    query_slots = queries.reshape(segment_length, ulysses_width, head_width)
    grad_slots = out_grad.reshape(segment_length, ulysses_width, head_width)
    kv_local = jnp.concatenate(
        [
            key_vector_rows.reshape(segment_length, KEY_VALUE_HEADS, HEAD_SIZE),
            value_vector_rows.reshape(segment_length, KEY_VALUE_HEADS, HEAD_SIZE),
        ],
        axis=2,
    )
    kv_slots = jnp.repeat(kv_local, copy_count, axis=1)
    query_all, kv_mine, grad_all = (
        lax.all_to_all(query_slots, "uly", split_axis=1, concat_axis=0, tiled=True),
        lax.all_to_all(kv_slots, "uly", split_axis=1, concat_axis=0, tiled=True),
        lax.all_to_all(grad_slots, "uly", split_axis=1, concat_axis=0, tiled=True),
    )
    keys_all = lax.all_gather(kv_mine[:, 0, :], ("chip", "core"), axis=0, tiled=True)
    item_count = heads_dev * ulysses_width
    item_ids = jnp.arange(item_count, dtype=jnp.int32)
    head_ids = item_ids // ulysses_width
    slot_ids = item_ids % ulysses_width
    first_pos = (slot_ids * cycle_size + cycle_index) * segment_length
    entries = block_list[head_ids, first_pos // BLOCK]
    earlier = jnp.arange(list_len)[:, None] > jnp.arange(list_len)[None, :]
    repeated = jnp.any((entries[:, :, None] == entries[:, None, :]) & earlier[None, :, :], axis=2)
    key_base = jnp.where(repeated, 1 << 30, entries * BLOCK)
    units_per_block = BLOCK // segment_length
    natural_segs = (
        entries[:, :, None] * units_per_block
        + jnp.arange(units_per_block, dtype=jnp.int32)[None, None, :]
    )
    canon_rows = (
        natural_segs % cycle_size * ulysses_width + natural_segs // cycle_size
    ) * segment_length
    half_slots = ulysses_width // 2
    seg_owner = natural_segs % cycle_size
    seg_slot = natural_segs // cycle_size
    plane_rows = chip_count * half_slots * segment_length
    grad_rows = (
        seg_slot // half_slots * core_count + (seg_owner % core_count - core_index) % core_count
    ) * plane_rows + (
        seg_owner // core_count * half_slots + seg_slot % half_slots
    ) * segment_length
    table = jnp.concatenate(
        [
            first_pos.reshape(-1),
            key_base.reshape(-1),
            canon_rows.reshape(-1),
            grad_rows.reshape(-1),
        ]
    ).astype(jnp.int32)
    q_rows = query_all.reshape(ulysses_width * segment_length, head_width)
    g_rows = grad_all.reshape(ulysses_width * segment_length, head_width)
    common = dict(
        heads_dev=heads_dev,
        slots=ulysses_width,
        seg_len=segment_length,
        list_len=list_len,
        units_per_block=units_per_block,
        score_scale=score_scale,
    )
    plane_shape = jax.ShapeDtypeStruct((core_count, plane_rows, 2 * HEAD_SIZE), jnp.float32)
    high_count = ulysses_width - half_slots
    part_rows = jax.ShapeDtypeStruct((high_count * segment_length, head_width), jnp.bfloat16)
    low_rows = jax.ShapeDtypeStruct((half_slots * segment_length, head_width), jnp.bfloat16)
    vmem = pl.BlockSpec(memory_space=pltpu.VMEM)
    smem = pl.BlockSpec(memory_space=pltpu.SMEM)
    scratch = [pltpu.VMEM((list_len * BLOCK, 2 * HEAD_SIZE), jnp.bfloat16)]
    params = pltpu.CompilerParams(vmem_limit_bytes=48 * 1024 * 1024)
    out_high, qgrad_high, low_part, high_part = pl.pallas_call(
        functools.partial(
            attention_kernel, first_slot=half_slots, slot_count=high_count, carry_low=False, **common
        ),
        out_shape=(part_rows, part_rows, plane_shape, plane_shape),
        in_specs=[smem, vmem, vmem, vmem],
        out_specs=(vmem, vmem, vmem, vmem),
        scratch_shapes=scratch,
        compiler_params=params,
    )(table, q_rows, g_rows, keys_all)
    pair = [(0, 1), (1, 0)]
    high_sum = (high_part[0] + lax.ppermute(high_part[1], "core", pair)).reshape(
        chip_count, half_slots * segment_length, 2 * HEAD_SIZE
    )
    high_sum, low_part = lax.optimization_barrier((high_sum, low_part))
    owned_high = lax.psum_scatter(high_sum, "chip", scatter_dimension=0, tiled=True)
    out_low, qgrad_low, low_total = pl.pallas_call(
        functools.partial(
            attention_kernel, first_slot=0, slot_count=half_slots, carry_low=True, **common
        ),
        out_shape=(low_rows, low_rows, plane_shape),
        in_specs=[smem, vmem, vmem, vmem, vmem],
        out_specs=(vmem, vmem, vmem),
        scratch_shapes=scratch,
        compiler_params=params,
    )(table, q_rows, g_rows, keys_all, low_part)
    low_sum = (low_total[0] + lax.ppermute(low_total[1], "core", pair)).reshape(
        chip_count, half_slots * segment_length, 2 * HEAD_SIZE
    )
    owned_low = lax.psum_scatter(low_sum, "chip", scatter_dimension=0, tiled=True)
    owned = jnp.concatenate([owned_low, owned_high], axis=1)
    out_rows = jnp.concatenate([out_low, out_high], axis=0)
    qgrad_rows = jnp.concatenate([qgrad_low, qgrad_high], axis=0)
    out_items = out_rows.reshape(ulysses_width * segment_length, 1, head_width)
    qgrad_items = qgrad_rows.reshape(ulysses_width * segment_length, 1, head_width)
    attended_back, qgrad_back = (
        lax.all_to_all(out_items, "uly", split_axis=0, concat_axis=1, tiled=True),
        lax.all_to_all(qgrad_items, "uly", split_axis=0, concat_axis=1, tiled=True),
    )
    attended = attended_back.reshape(segment_length, ulysses_width * head_width)
    query_grad = qgrad_back.reshape(segment_length, ulysses_width * head_width)
    result_tuple = lax.all_to_all(
        owned.reshape(ulysses_width * segment_length, 1, 2 * HEAD_SIZE),
        "uly",
        split_axis=0,
        concat_axis=1,
        tiled=True,
    )
    summed_total = result_tuple.reshape(
        segment_length, KEY_VALUE_HEADS, copy_count, 2 * HEAD_SIZE
    ).sum(axis=2)
    gradient_keys = (
        summed_total[:, :, :HEAD_SIZE]
        .reshape(segment_length, KEY_VALUE_HEADS * HEAD_SIZE)
        .astype(jnp.bfloat16)
    )
    gradient_values = (
        summed_total[:, :, HEAD_SIZE:]
        .reshape(segment_length, KEY_VALUE_HEADS * HEAD_SIZE)
        .astype(jnp.bfloat16)
    )
    return (attended, query_grad, gradient_keys, gradient_values)


def solution(mesh):
    devices = mesh.devices
    cores = 2
    fine_mesh = Mesh(
        devices.reshape(devices.shape[0], devices.shape[1] // cores, cores), ("uly", "chip", "core")
    )
    rows = P(("uly", "chip", "core"), None)
    in_specs = (rows, rows, rows, rows, P("uly", None, None))
    out_specs = (rows, rows, rows, rows)
    return jax.shard_map(body, mesh=fine_mesh, in_specs=in_specs, out_specs=out_specs, check_vma=False)
```

```python
import functools
import math

import jax
import jax.numpy as jnp
from jax import lax
from jax.experimental import pallas as pl
from jax.experimental.pallas import tpu as pltpu
from jax.sharding import Mesh, PartitionSpec as P

KEY_VALUE_HEADS = 2
HEAD_SIZE = 128
BLOCK = 128


def attention_kernel(
    tab_ref, q_ref, g_ref, pq_ref, pg_ref, kv_ref, out_ref, dq_ref, dkv_ref, kvg_ref,
    *, heads_dev, slots, seg_len, list_len, units_per_block, score_scale,
):
    dkv_ref[...] = jnp.zeros(dkv_ref.shape, jnp.float32)
    n_items = 2 * heads_dev * slots
    key_len = list_len * BLOCK
    base_at = n_items
    rows_at = n_items + n_items * list_len
    grad_at = rows_at + n_items * list_len * units_per_block
    lane = lax.broadcasted_iota(jnp.int32, (1, key_len), 1)
    lane_block = lane // BLOCK
    lane_offset = lane % BLOCK
    query_offset = lax.broadcasted_iota(jnp.int32, (seg_len, 1), 0)
    nt = (((1,), (1,)), ((), ()))
    tn = (((0,), (0,)), ((), ()))
    sources = ((q_ref, g_ref, True), (pq_ref, pg_ref, False))
    for source, (sq_ref, sg_ref, own) in enumerate(sources):
      for head in range(heads_dev):
        cols = slice(head * HEAD_SIZE, (head + 1) * HEAD_SIZE)

        def item_step(slot, carry, head=head, cols=cols, source=source, sq_ref=sq_ref, sg_ref=sg_ref, own=own):
            item = (source * heads_dev + head) * slots + slot
            rows = pl.ds(pl.multiple_of(slot * seg_len, seg_len), seg_len)
            query_block = sq_ref[rows, cols]
            grad_block = sg_ref[rows, cols]
            key_pos = lane_offset
            base = jnp.zeros((1, key_len), jnp.int32)
            for j in range(list_len):
                base = jnp.where(lane_block == j, tab_ref[base_at + item * list_len + j], base)
                for u in range(units_per_block):
                    src = tab_ref[rows_at + (item * list_len + j) * units_per_block + u]
                    kvg_ref[pl.ds(j * BLOCK + u * seg_len, seg_len), :] = kv_ref[
                        pl.ds(pl.multiple_of(src, seg_len), seg_len), :
                    ]
            key_pos = base + lane_offset
            query_pos = tab_ref[item] + query_offset
            allowed = key_pos <= query_pos
            key_group = kvg_ref[:, :HEAD_SIZE]
            value_group = kvg_ref[:, HEAD_SIZE:]
            scores = (
                lax.dot_general(query_block, key_group, nt, preferred_element_type=jnp.float32)
                * score_scale
            )
            masked = jnp.where(allowed, scores, -1e30)
            row_max = jnp.max(masked, axis=1, keepdims=True)
            row_sum = jnp.sum(
                jnp.where(allowed, jnp.exp(masked - row_max), 0.0), axis=1, keepdims=True
            )
            log_sum = row_max + jnp.log(row_sum)
            weights = jnp.where(allowed, jnp.exp(masked - log_sum), 0.0)
            weights_low = weights.astype(jnp.bfloat16)
            out_block = jnp.dot(
                weights_low, value_group, preferred_element_type=jnp.float32
            ).astype(jnp.bfloat16)
            if own:
                out_ref[rows, cols] = out_block
            row_dot = jnp.sum(
                grad_block.astype(jnp.float32) * out_block.astype(jnp.float32),
                axis=1,
                keepdims=True,
            )
            grad_weights = lax.dot_general(
                grad_block, value_group, nt, preferred_element_type=jnp.float32
            )
            score_grad = (weights * (grad_weights - row_dot) * score_scale).astype(jnp.bfloat16)
            if own:
                dq_ref[rows, cols] = jnp.dot(
                    score_grad, key_group, preferred_element_type=jnp.float32
                ).astype(jnp.bfloat16)
            key_part = lax.dot_general(score_grad, query_block, tn, preferred_element_type=jnp.float32)
            value_part = lax.dot_general(weights_low, grad_block, tn, preferred_element_type=jnp.float32)
            for j in range(list_len):
                for u in range(units_per_block):
                    dst = tab_ref[grad_at + (item * list_len + j) * units_per_block + u]
                    dst_rows = pl.ds(pl.multiple_of(jnp.maximum(dst, 0), seg_len), seg_len)
                    lo = j * BLOCK + u * seg_len
                    key_rows = key_part[lo : lo + seg_len]
                    value_rows = value_part[lo : lo + seg_len]

                    @pl.when(dst >= 0)
                    def _(dst_rows=dst_rows, key_rows=key_rows, value_rows=value_rows):
                        dkv_ref[dst_rows, :HEAD_SIZE] += key_rows
                        dkv_ref[dst_rows, HEAD_SIZE:] += value_rows
            return carry

        lax.fori_loop(0, slots, item_step, 0)


def body(queries, key_vector_rows, value_vector_rows, out_grad, block_list):
    ulysses_width = lax.axis_size("uly")
    core_count = lax.axis_size("core")
    chip_count = lax.axis_size("chip")
    cycle_size = chip_count * core_count
    segment_length = queries.shape[0]
    heads_dev = block_list.shape[0]
    list_len = block_list.shape[2]
    head_width = heads_dev * HEAD_SIZE
    copy_count = ulysses_width // KEY_VALUE_HEADS
    core_index = lax.axis_index("core")
    cycle_index = lax.axis_index("chip") * core_count + core_index
    score_scale = 1.0 / math.sqrt(HEAD_SIZE)
    sub_length = min(segment_length, BLOCK)
    sub_count = segment_length // sub_length
    unit_len = min(segment_length, BLOCK)
    units_per_block = BLOCK // unit_len
    units_per_segment = segment_length // unit_len
    total_tokens = segment_length * ulysses_width * cycle_size
    units_total = total_tokens // unit_len
    query_slots = queries.reshape(segment_length, ulysses_width, head_width)
    grad_slots = out_grad.reshape(segment_length, ulysses_width, head_width)
    kv_local = jnp.concatenate(
        [
            key_vector_rows.reshape(segment_length, KEY_VALUE_HEADS, HEAD_SIZE),
            value_vector_rows.reshape(segment_length, KEY_VALUE_HEADS, HEAD_SIZE),
        ],
        axis=2,
    )
    kv_slots = jnp.repeat(kv_local, copy_count, axis=1)
    query_all, kv_mine, grad_all = (
        lax.all_to_all(query_slots, "uly", split_axis=1, concat_axis=0, tiled=True),
        lax.all_to_all(kv_slots, "uly", split_axis=1, concat_axis=0, tiled=True),
        lax.all_to_all(grad_slots, "uly", split_axis=1, concat_axis=0, tiled=True),
    )
    keys_all = lax.all_gather(kv_mine[:, 0, :], ("chip", "core"), axis=0, tiled=True)
    item_count = heads_dev * ulysses_width
    item_ids = jnp.arange(item_count, dtype=jnp.int32)
    head_ids = item_ids // ulysses_width
    slot_ids = item_ids % ulysses_width
    earlier = jnp.arange(list_len)[:, None] > jnp.arange(list_len)[None, :]
    units_per_block = BLOCK // segment_length
    chip_index = lax.axis_index("chip")

    def item_table(source_core):
        first_pos = (slot_ids * cycle_size + chip_index * core_count + source_core) * segment_length
        entries = block_list[head_ids, first_pos // BLOCK]
        repeated = jnp.any(
            (entries[:, :, None] == entries[:, None, :]) & earlier[None, :, :], axis=2
        )
        key_base = jnp.where(repeated, 1 << 30, entries * BLOCK)
        natural_segs = (
            entries[:, :, None] * units_per_block
            + jnp.arange(units_per_block, dtype=jnp.int32)[None, None, :]
        )
        canon_rows = (
            natural_segs % cycle_size * ulysses_width + natural_segs // cycle_size
        ) * segment_length
        seg_owner = natural_segs % cycle_size
        grad_rows = jnp.where(
            seg_owner % core_count == core_index,
            (seg_owner // core_count * ulysses_width + natural_segs // cycle_size) * segment_length,
            -1,
        )
        return first_pos, key_base, canon_rows, grad_rows

    mine = item_table(core_index)
    peer = item_table(1 - core_index)
    table = jnp.concatenate(
        [jnp.concatenate([a.reshape(-1), b.reshape(-1)]) for a, b in zip(mine, peer)]
    ).astype(jnp.int32)
    q_rows = query_all.reshape(ulysses_width * segment_length, head_width)
    g_rows = grad_all.reshape(ulysses_width * segment_length, head_width)
    pair = [(0, 1), (1, 0)]
    peer_q, peer_g = lax.ppermute((q_rows, g_rows), "core", pair)
    kernel = functools.partial(
        attention_kernel,
        heads_dev=heads_dev,
        slots=ulysses_width,
        seg_len=segment_length,
        list_len=list_len,
        units_per_block=units_per_block,
        score_scale=score_scale,
    )
    out_rows, qgrad_rows, kv_grad_all = pl.pallas_call(
        kernel,
        out_shape=(
            jax.ShapeDtypeStruct(q_rows.shape, jnp.bfloat16),
            jax.ShapeDtypeStruct(q_rows.shape, jnp.bfloat16),
            jax.ShapeDtypeStruct(
                (keys_all.shape[0] // core_count, keys_all.shape[1]), jnp.float32
            ),
        ),
        in_specs=[pl.BlockSpec(memory_space=pltpu.SMEM)]
        + [pl.BlockSpec(memory_space=pltpu.VMEM)] * 5,
        out_specs=(
            pl.BlockSpec(memory_space=pltpu.VMEM),
            pl.BlockSpec(memory_space=pltpu.VMEM),
            pl.BlockSpec(memory_space=pltpu.VMEM),
        ),
        scratch_shapes=[pltpu.VMEM((list_len * BLOCK, 2 * HEAD_SIZE), jnp.bfloat16)],
        compiler_params=pltpu.CompilerParams(vmem_limit_bytes=48 * 1024 * 1024),
    )(table, q_rows, g_rows, peer_q, peer_g, keys_all)
    out_items = out_rows.reshape(ulysses_width * segment_length, 1, head_width)
    qgrad_items = qgrad_rows.reshape(ulysses_width * segment_length, 1, head_width)
    attended_back, qgrad_back = (
        lax.all_to_all(out_items, "uly", split_axis=0, concat_axis=1, tiled=True),
        lax.all_to_all(qgrad_items, "uly", split_axis=0, concat_axis=1, tiled=True),
    )
    attended = attended_back.reshape(segment_length, ulysses_width * head_width)
    query_grad = qgrad_back.reshape(segment_length, ulysses_width * head_width)
    chip_part = kv_grad_all.reshape(chip_count, ulysses_width * segment_length, 2 * HEAD_SIZE)
    owned = lax.psum_scatter(chip_part, "chip", scatter_dimension=0, tiled=True)
    result_tuple = lax.all_to_all(
        owned.reshape(ulysses_width * segment_length, 1, 2 * HEAD_SIZE),
        "uly",
        split_axis=0,
        concat_axis=1,
        tiled=True,
    )
    summed_total = result_tuple.reshape(
        segment_length, KEY_VALUE_HEADS, copy_count, 2 * HEAD_SIZE
    ).sum(axis=2)
    gradient_keys = (
        summed_total[:, :, :HEAD_SIZE]
        .reshape(segment_length, KEY_VALUE_HEADS * HEAD_SIZE)
        .astype(jnp.bfloat16)
    )
    gradient_values = (
        summed_total[:, :, HEAD_SIZE:]
        .reshape(segment_length, KEY_VALUE_HEADS * HEAD_SIZE)
        .astype(jnp.bfloat16)
    )
    return (attended, query_grad, gradient_keys, gradient_values)


def solution(mesh):
    devices = mesh.devices
    cores = 2
    fine_mesh = Mesh(
        devices.reshape(devices.shape[0], devices.shape[1] // cores, cores), ("uly", "chip", "core")
    )
    rows = P(("uly", "chip", "core"), None)
    in_specs = (rows, rows, rows, rows, P("uly", None, None))
    out_specs = (rows, rows, rows, rows)
    return jax.shard_map(body, mesh=fine_mesh, in_specs=in_specs, out_specs=out_specs, check_vma=False)
```

```python
import functools
import math

import jax
import jax.numpy as jnp
from jax import lax
from jax.experimental import pallas as pl
from jax.experimental.pallas import tpu as pltpu
from jax.sharding import Mesh, PartitionSpec as P

KEY_VALUE_HEADS = 2
HEAD_SIZE = 128
BLOCK = 128


def attention_kernel(
    tab_ref, q_ref, g_ref, pq_ref, pg_ref, kv_ref, out_ref, dq_ref, dkv_ref, kvg_ref,
    *, heads_dev, slots, seg_len, list_len, units_per_block, score_scale,
):
    dkv_ref[...] = jnp.zeros(dkv_ref.shape, jnp.float32)
    n_items = 2 * heads_dev * slots
    key_len = list_len * BLOCK
    base_at = n_items
    rows_at = n_items + n_items * list_len
    grad_at = rows_at + n_items * list_len * units_per_block
    lane = lax.broadcasted_iota(jnp.int32, (1, key_len), 1)
    lane_block = lane // BLOCK
    lane_offset = lane % BLOCK
    query_offset = lax.broadcasted_iota(jnp.int32, (seg_len, 1), 0)
    nt = (((1,), (1,)), ((), ()))
    tn = (((0,), (0,)), ((), ()))
    sources = ((q_ref, g_ref, True), (pq_ref, pg_ref, False))
    for source, (sq_ref, sg_ref, own) in enumerate(sources):
      for head in range(heads_dev):
        cols = slice(head * HEAD_SIZE, (head + 1) * HEAD_SIZE)

        def item_step(slot, carry, head=head, cols=cols, source=source, sq_ref=sq_ref, sg_ref=sg_ref, own=own):
            item = (source * heads_dev + head) * slots + slot
            rows = pl.ds(pl.multiple_of(slot * seg_len, seg_len), seg_len)
            query_block = sq_ref[rows, cols]
            grad_block = sg_ref[rows, cols]
            key_pos = lane_offset
            base = jnp.zeros((1, key_len), jnp.int32)
            for j in range(list_len):
                base = jnp.where(lane_block == j, tab_ref[base_at + item * list_len + j], base)
                for u in range(units_per_block):
                    src = tab_ref[rows_at + (item * list_len + j) * units_per_block + u]
                    kvg_ref[pl.ds(j * BLOCK + u * seg_len, seg_len), :] = kv_ref[
                        pl.ds(pl.multiple_of(src, seg_len), seg_len), :
                    ]
            key_pos = base + lane_offset
            query_pos = tab_ref[item] + query_offset
            allowed = key_pos <= query_pos
            key_group = kvg_ref[:, :HEAD_SIZE]
            value_group = kvg_ref[:, HEAD_SIZE:]
            scores = (
                lax.dot_general(query_block, key_group, nt, preferred_element_type=jnp.float32)
                * score_scale
            )
            masked = jnp.where(allowed, scores, -1e30)
            row_max = jnp.max(masked, axis=1, keepdims=True)
            row_sum = jnp.sum(
                jnp.where(allowed, jnp.exp(masked - row_max), 0.0), axis=1, keepdims=True
            )
            log_sum = row_max + jnp.log(row_sum)
            weights = jnp.where(allowed, jnp.exp(masked - log_sum), 0.0)
            weights_low = weights.astype(jnp.bfloat16)
            out_block = jnp.dot(
                weights_low, value_group, preferred_element_type=jnp.float32
            ).astype(jnp.bfloat16)
            if own:
                out_ref[rows, cols] = out_block
            row_dot = jnp.sum(
                grad_block.astype(jnp.float32) * out_block.astype(jnp.float32),
                axis=1,
                keepdims=True,
            )
            grad_weights = lax.dot_general(
                grad_block, value_group, nt, preferred_element_type=jnp.float32
            )
            score_grad = (weights * (grad_weights - row_dot) * score_scale).astype(jnp.bfloat16)
            if own:
                dq_ref[rows, cols] = jnp.dot(
                    score_grad, key_group, preferred_element_type=jnp.float32
                ).astype(jnp.bfloat16)
            key_part = lax.dot_general(score_grad, query_block, tn, preferred_element_type=jnp.float32)
            value_part = lax.dot_general(weights_low, grad_block, tn, preferred_element_type=jnp.float32)
            for j in range(list_len):
                for u in range(units_per_block):
                    dst = tab_ref[grad_at + (item * list_len + j) * units_per_block + u]
                    dst_rows = pl.ds(pl.multiple_of(jnp.maximum(dst, 0), seg_len), seg_len)
                    lo = j * BLOCK + u * seg_len
                    key_rows = key_part[lo : lo + seg_len]
                    value_rows = value_part[lo : lo + seg_len]

                    @pl.when(dst >= 0)
                    def _(dst_rows=dst_rows, key_rows=key_rows, value_rows=value_rows):
                        dkv_ref[dst_rows, :HEAD_SIZE] += key_rows
                        dkv_ref[dst_rows, HEAD_SIZE:] += value_rows
            return carry

        lax.fori_loop(0, slots, item_step, 0)


def body(queries, key_vector_rows, value_vector_rows, out_grad, block_list):
    ulysses_width = lax.axis_size("uly")
    core_count = lax.axis_size("core")
    chip_count = lax.axis_size("chip")
    cycle_size = chip_count * core_count
    segment_length = queries.shape[0]
    heads_dev = block_list.shape[0]
    list_len = block_list.shape[2]
    head_width = heads_dev * HEAD_SIZE
    copy_count = ulysses_width // KEY_VALUE_HEADS
    core_index = lax.axis_index("core")
    cycle_index = lax.axis_index("chip") * core_count + core_index
    score_scale = 1.0 / math.sqrt(HEAD_SIZE)
    sub_length = min(segment_length, BLOCK)
    sub_count = segment_length // sub_length
    unit_len = min(segment_length, BLOCK)
    units_per_block = BLOCK // unit_len
    units_per_segment = segment_length // unit_len
    total_tokens = segment_length * ulysses_width * cycle_size
    units_total = total_tokens // unit_len
    query_slots = queries.reshape(segment_length, ulysses_width, head_width)
    grad_slots = out_grad.reshape(segment_length, ulysses_width, head_width)
    kv_local = jnp.concatenate(
        [
            key_vector_rows.reshape(segment_length, KEY_VALUE_HEADS, HEAD_SIZE),
            value_vector_rows.reshape(segment_length, KEY_VALUE_HEADS, HEAD_SIZE),
        ],
        axis=2,
    )
    kv_slots = jnp.repeat(kv_local, copy_count, axis=1)
    query_all, kv_mine, grad_all = (
        lax.all_to_all(query_slots, "uly", split_axis=1, concat_axis=0, tiled=True),
        lax.all_to_all(kv_slots, "uly", split_axis=1, concat_axis=0, tiled=True),
        lax.all_to_all(grad_slots, "uly", split_axis=1, concat_axis=0, tiled=True),
    )
    keys_all = lax.all_gather(kv_mine[:, 0, :], ("chip", "core"), axis=0, tiled=True)
    item_count = heads_dev * ulysses_width
    item_ids = jnp.arange(item_count, dtype=jnp.int32)
    head_ids = item_ids // ulysses_width
    slot_ids = item_ids % ulysses_width
    earlier = jnp.arange(list_len)[:, None] > jnp.arange(list_len)[None, :]
    units_per_block = BLOCK // segment_length
    chip_index = lax.axis_index("chip")

    def item_table(source_core):
        first_pos = (slot_ids * cycle_size + chip_index * core_count + source_core) * segment_length
        entries = block_list[head_ids, first_pos // BLOCK]
        repeated = jnp.any(
            (entries[:, :, None] == entries[:, None, :]) & earlier[None, :, :], axis=2
        )
        key_base = jnp.where(repeated, 1 << 30, entries * BLOCK)
        natural_segs = (
            entries[:, :, None] * units_per_block
            + jnp.arange(units_per_block, dtype=jnp.int32)[None, None, :]
        )
        canon_rows = (
            natural_segs % cycle_size * ulysses_width + natural_segs // cycle_size
        ) * segment_length
        seg_owner = natural_segs % cycle_size
        grad_rows = jnp.where(
            seg_owner % core_count == core_index,
            (seg_owner // core_count * ulysses_width + natural_segs // cycle_size) * segment_length,
            -1,
        )
        return first_pos, key_base, canon_rows, grad_rows

    mine = item_table(core_index)
    peer = item_table(1 - core_index)
    table = jnp.concatenate(
        [jnp.concatenate([a.reshape(-1), b.reshape(-1)]) for a, b in zip(mine, peer)]
    ).astype(jnp.int32)
    q_rows = query_all.reshape(ulysses_width * segment_length, head_width)
    g_rows = grad_all.reshape(ulysses_width * segment_length, head_width)
    pair = [(0, 1), (1, 0)]
    peer_q, peer_g = lax.ppermute((q_rows, g_rows), "core", pair)
    kernel = functools.partial(
        attention_kernel,
        heads_dev=heads_dev,
        slots=ulysses_width,
        seg_len=segment_length,
        list_len=list_len,
        units_per_block=units_per_block,
        score_scale=score_scale,
    )
    out_rows, qgrad_rows, kv_grad_all = pl.pallas_call(
        kernel,
        out_shape=(
            jax.ShapeDtypeStruct(q_rows.shape, jnp.bfloat16),
            jax.ShapeDtypeStruct(q_rows.shape, jnp.bfloat16),
            jax.ShapeDtypeStruct(
                (keys_all.shape[0] // core_count, keys_all.shape[1]), jnp.float32
            ),
        ),
        in_specs=[pl.BlockSpec(memory_space=pltpu.SMEM)]
        + [pl.BlockSpec(memory_space=pltpu.VMEM)] * 5,
        out_specs=(
            pl.BlockSpec(memory_space=pltpu.VMEM),
            pl.BlockSpec(memory_space=pltpu.VMEM),
            pl.BlockSpec(memory_space=pltpu.VMEM),
        ),
        scratch_shapes=[pltpu.VMEM((list_len * BLOCK, 2 * HEAD_SIZE), jnp.bfloat16)],
        compiler_params=pltpu.CompilerParams(vmem_limit_bytes=48 * 1024 * 1024),
    )(table, q_rows, g_rows, peer_q, peer_g, keys_all)
    out_items = out_rows.reshape(ulysses_width * segment_length, 1, head_width)
    qgrad_items = qgrad_rows.reshape(ulysses_width * segment_length, 1, head_width)
    attended_back, qgrad_back = (
        lax.all_to_all(out_items, "uly", split_axis=0, concat_axis=1, tiled=True),
        lax.all_to_all(qgrad_items, "uly", split_axis=0, concat_axis=1, tiled=True),
    )
    attended = attended_back.reshape(segment_length, ulysses_width * head_width)
    query_grad = qgrad_back.reshape(segment_length, ulysses_width * head_width)
    chip_part = kv_grad_all.reshape(chip_count, ulysses_width * segment_length, 2 * HEAD_SIZE)
    owned = lax.all_to_all(chip_part, "chip", split_axis=0, concat_axis=0, tiled=True).sum(
        axis=0, keepdims=True
    )
    result_tuple = lax.all_to_all(
        owned.reshape(ulysses_width * segment_length, 1, 2 * HEAD_SIZE),
        "uly",
        split_axis=0,
        concat_axis=1,
        tiled=True,
    )
    summed_total = result_tuple.reshape(
        segment_length, KEY_VALUE_HEADS, copy_count, 2 * HEAD_SIZE
    ).sum(axis=2)
    gradient_keys = (
        summed_total[:, :, :HEAD_SIZE]
        .reshape(segment_length, KEY_VALUE_HEADS * HEAD_SIZE)
        .astype(jnp.bfloat16)
    )
    gradient_values = (
        summed_total[:, :, HEAD_SIZE:]
        .reshape(segment_length, KEY_VALUE_HEADS * HEAD_SIZE)
        .astype(jnp.bfloat16)
    )
    return (attended, query_grad, gradient_keys, gradient_values)


def solution(mesh):
    devices = mesh.devices
    cores = 2
    fine_mesh = Mesh(
        devices.reshape(devices.shape[0], devices.shape[1] // cores, cores), ("uly", "chip", "core")
    )
    rows = P(("uly", "chip", "core"), None)
    in_specs = (rows, rows, rows, rows, P("uly", None, None))
    out_specs = (rows, rows, rows, rows)
    return jax.shard_map(body, mesh=fine_mesh, in_specs=in_specs, out_specs=out_specs, check_vma=False)
```

```python
import functools
import math

import jax
import jax.numpy as jnp
from jax import lax
from jax.experimental import pallas as pl
from jax.experimental.pallas import tpu as pltpu
from jax.sharding import Mesh, PartitionSpec as P

KEY_VALUE_HEADS = 2
HEAD_SIZE = 128
BLOCK = 128


def attention_kernel(
    tab_ref, q_ref, g_ref, pq_ref, pg_ref, kv_hbm, out_ref, dq_ref, dkv_ref, kvg_ref, sem,
    *, heads_dev, slots, seg_len, list_len, units_per_block, score_scale,
):
    dkv_ref[...] = jnp.zeros(dkv_ref.shape, jnp.float32)
    n_items = 2 * heads_dev * slots
    key_len = list_len * BLOCK
    base_at = n_items
    rows_at = n_items + n_items * list_len
    grad_at = rows_at + n_items * list_len * units_per_block
    lane = lax.broadcasted_iota(jnp.int32, (1, key_len), 1)
    lane_block = lane // BLOCK
    lane_offset = lane % BLOCK
    query_offset = lax.broadcasted_iota(jnp.int32, (seg_len, 1), 0)
    nt = (((1,), (1,)), ((), ()))
    tn = (((0,), (0,)), ((), ()))
    sources = ((q_ref, g_ref, True), (pq_ref, pg_ref, False))

    def fetch(item, buf):
        for j in range(list_len):
            for u in range(units_per_block):
                src = tab_ref[rows_at + (item * list_len + j) * units_per_block + u]
                pltpu.make_async_copy(
                    kv_hbm.at[pl.ds(pl.multiple_of(src, seg_len), seg_len)],
                    kvg_ref.at[buf, pl.ds(j * BLOCK + u * seg_len, seg_len)],
                    sem.at[buf],
                ).start()

    def wait_all(buf):
        pltpu.make_async_copy(kv_hbm.at[pl.ds(0, key_len)], kvg_ref.at[buf], sem.at[buf]).wait()

    fetch(0, 0)
    for source, (sq_ref, sg_ref, own) in enumerate(sources):
      for head in range(heads_dev):
        cols = slice(head * HEAD_SIZE, (head + 1) * HEAD_SIZE)

        def item_step(slot, carry, head=head, cols=cols, source=source, sq_ref=sq_ref, sg_ref=sg_ref, own=own):
            item = (source * heads_dev + head) * slots + slot
            buf = item % 2
            wait_all(buf)

            @pl.when(item + 1 < n_items)
            def _():
                fetch(item + 1, 1 - buf)
            rows = pl.ds(pl.multiple_of(slot * seg_len, seg_len), seg_len)
            query_block = sq_ref[rows, cols]
            grad_block = sg_ref[rows, cols]
            key_pos = lane_offset
            base = jnp.zeros((1, key_len), jnp.int32)
            for j in range(list_len):
                base = jnp.where(lane_block == j, tab_ref[base_at + item * list_len + j], base)
            key_pos = base + lane_offset
            query_pos = tab_ref[item] + query_offset
            allowed = key_pos <= query_pos
            key_group = kvg_ref[buf, :, :HEAD_SIZE]
            value_group = kvg_ref[buf, :, HEAD_SIZE:]
            scores = (
                lax.dot_general(query_block, key_group, nt, preferred_element_type=jnp.float32)
                * score_scale
            )
            masked = jnp.where(allowed, scores, -1e30)
            row_max = jnp.max(masked, axis=1, keepdims=True)
            row_sum = jnp.sum(
                jnp.where(allowed, jnp.exp(masked - row_max), 0.0), axis=1, keepdims=True
            )
            log_sum = row_max + jnp.log(row_sum)
            weights = jnp.where(allowed, jnp.exp(masked - log_sum), 0.0)
            weights_low = weights.astype(jnp.bfloat16)
            out_block = jnp.dot(
                weights_low, value_group, preferred_element_type=jnp.float32
            ).astype(jnp.bfloat16)
            if own:
                out_ref[rows, cols] = out_block
            row_dot = jnp.sum(
                grad_block.astype(jnp.float32) * out_block.astype(jnp.float32),
                axis=1,
                keepdims=True,
            )
            grad_weights = lax.dot_general(
                grad_block, value_group, nt, preferred_element_type=jnp.float32
            )
            score_grad = (weights * (grad_weights - row_dot) * score_scale).astype(jnp.bfloat16)
            if own:
                dq_ref[rows, cols] = jnp.dot(
                    score_grad, key_group, preferred_element_type=jnp.float32
                ).astype(jnp.bfloat16)
            key_part = lax.dot_general(score_grad, query_block, tn, preferred_element_type=jnp.float32)
            value_part = lax.dot_general(weights_low, grad_block, tn, preferred_element_type=jnp.float32)
            for j in range(list_len):
                for u in range(units_per_block):
                    dst = tab_ref[grad_at + (item * list_len + j) * units_per_block + u]
                    dst_rows = pl.ds(pl.multiple_of(jnp.maximum(dst, 0), seg_len), seg_len)
                    lo = j * BLOCK + u * seg_len
                    key_rows = key_part[lo : lo + seg_len]
                    value_rows = value_part[lo : lo + seg_len]

                    @pl.when(dst >= 0)
                    def _(dst_rows=dst_rows, key_rows=key_rows, value_rows=value_rows):
                        dkv_ref[dst_rows, :HEAD_SIZE] += key_rows
                        dkv_ref[dst_rows, HEAD_SIZE:] += value_rows
            return carry

        lax.fori_loop(0, slots, item_step, 0)


def body(queries, key_vector_rows, value_vector_rows, out_grad, block_list):
    ulysses_width = lax.axis_size("uly")
    core_count = lax.axis_size("core")
    chip_count = lax.axis_size("chip")
    cycle_size = chip_count * core_count
    segment_length = queries.shape[0]
    heads_dev = block_list.shape[0]
    list_len = block_list.shape[2]
    head_width = heads_dev * HEAD_SIZE
    copy_count = ulysses_width // KEY_VALUE_HEADS
    core_index = lax.axis_index("core")
    cycle_index = lax.axis_index("chip") * core_count + core_index
    score_scale = 1.0 / math.sqrt(HEAD_SIZE)
    sub_length = min(segment_length, BLOCK)
    sub_count = segment_length // sub_length
    unit_len = min(segment_length, BLOCK)
    units_per_block = BLOCK // unit_len
    units_per_segment = segment_length // unit_len
    total_tokens = segment_length * ulysses_width * cycle_size
    units_total = total_tokens // unit_len
    query_slots = queries.reshape(segment_length, ulysses_width, head_width)
    grad_slots = out_grad.reshape(segment_length, ulysses_width, head_width)
    kv_local = jnp.concatenate(
        [
            key_vector_rows.reshape(segment_length, KEY_VALUE_HEADS, HEAD_SIZE),
            value_vector_rows.reshape(segment_length, KEY_VALUE_HEADS, HEAD_SIZE),
        ],
        axis=2,
    )
    kv_slots = jnp.repeat(kv_local, copy_count, axis=1)
    query_all, kv_mine, grad_all = (
        lax.all_to_all(query_slots, "uly", split_axis=1, concat_axis=0, tiled=True),
        lax.all_to_all(kv_slots, "uly", split_axis=1, concat_axis=0, tiled=True),
        lax.all_to_all(grad_slots, "uly", split_axis=1, concat_axis=0, tiled=True),
    )
    keys_all = lax.all_gather(kv_mine[:, 0, :], ("chip", "core"), axis=0, tiled=True)
    item_count = heads_dev * ulysses_width
    item_ids = jnp.arange(item_count, dtype=jnp.int32)
    head_ids = item_ids // ulysses_width
    slot_ids = item_ids % ulysses_width
    earlier = jnp.arange(list_len)[:, None] > jnp.arange(list_len)[None, :]
    units_per_block = BLOCK // segment_length
    chip_index = lax.axis_index("chip")

    def item_table(source_core):
        first_pos = (slot_ids * cycle_size + chip_index * core_count + source_core) * segment_length
        entries = block_list[head_ids, first_pos // BLOCK]
        repeated = jnp.any(
            (entries[:, :, None] == entries[:, None, :]) & earlier[None, :, :], axis=2
        )
        key_base = jnp.where(repeated, 1 << 30, entries * BLOCK)
        natural_segs = (
            entries[:, :, None] * units_per_block
            + jnp.arange(units_per_block, dtype=jnp.int32)[None, None, :]
        )
        canon_rows = (
            natural_segs % cycle_size * ulysses_width + natural_segs // cycle_size
        ) * segment_length
        seg_owner = natural_segs % cycle_size
        grad_rows = jnp.where(
            seg_owner % core_count == core_index,
            (seg_owner // core_count * ulysses_width + natural_segs // cycle_size) * segment_length,
            -1,
        )
        return first_pos, key_base, canon_rows, grad_rows

    mine = item_table(core_index)
    peer = item_table(1 - core_index)
    table = jnp.concatenate(
        [jnp.concatenate([a.reshape(-1), b.reshape(-1)]) for a, b in zip(mine, peer)]
    ).astype(jnp.int32)
    q_rows = query_all.reshape(ulysses_width * segment_length, head_width)
    g_rows = grad_all.reshape(ulysses_width * segment_length, head_width)
    pair = [(0, 1), (1, 0)]
    peer_q, peer_g = lax.ppermute((q_rows, g_rows), "core", pair)
    kernel = functools.partial(
        attention_kernel,
        heads_dev=heads_dev,
        slots=ulysses_width,
        seg_len=segment_length,
        list_len=list_len,
        units_per_block=units_per_block,
        score_scale=score_scale,
    )
    out_rows, qgrad_rows, kv_grad_all = pl.pallas_call(
        kernel,
        out_shape=(
            jax.ShapeDtypeStruct(q_rows.shape, jnp.bfloat16),
            jax.ShapeDtypeStruct(q_rows.shape, jnp.bfloat16),
            jax.ShapeDtypeStruct(
                (keys_all.shape[0] // core_count, keys_all.shape[1]), jnp.float32
            ),
        ),
        in_specs=[pl.BlockSpec(memory_space=pltpu.SMEM)]
        + [pl.BlockSpec(memory_space=pltpu.VMEM)] * 4
        + [pl.BlockSpec(memory_space=pl.ANY)],
        out_specs=(
            pl.BlockSpec(memory_space=pltpu.VMEM),
            pl.BlockSpec(memory_space=pltpu.VMEM),
            pl.BlockSpec(memory_space=pltpu.VMEM),
        ),
        scratch_shapes=[
            pltpu.VMEM((2, list_len * BLOCK, 2 * HEAD_SIZE), jnp.bfloat16),
            pltpu.SemaphoreType.DMA((2,)),
        ],
        compiler_params=pltpu.CompilerParams(vmem_limit_bytes=48 * 1024 * 1024),
    )(table, q_rows, g_rows, peer_q, peer_g, keys_all)
    out_items = out_rows.reshape(ulysses_width * segment_length, 1, head_width)
    qgrad_items = qgrad_rows.reshape(ulysses_width * segment_length, 1, head_width)
    attended_back, qgrad_back = (
        lax.all_to_all(out_items, "uly", split_axis=0, concat_axis=1, tiled=True),
        lax.all_to_all(qgrad_items, "uly", split_axis=0, concat_axis=1, tiled=True),
    )
    attended = attended_back.reshape(segment_length, ulysses_width * head_width)
    query_grad = qgrad_back.reshape(segment_length, ulysses_width * head_width)
    chip_part = kv_grad_all.reshape(chip_count, ulysses_width * segment_length, 2 * HEAD_SIZE)
    owned = lax.psum_scatter(chip_part, "chip", scatter_dimension=0, tiled=True)
    result_tuple = lax.all_to_all(
        owned.reshape(ulysses_width * segment_length, 1, 2 * HEAD_SIZE),
        "uly",
        split_axis=0,
        concat_axis=1,
        tiled=True,
    )
    summed_total = result_tuple.reshape(
        segment_length, KEY_VALUE_HEADS, copy_count, 2 * HEAD_SIZE
    ).sum(axis=2)
    gradient_keys = (
        summed_total[:, :, :HEAD_SIZE]
        .reshape(segment_length, KEY_VALUE_HEADS * HEAD_SIZE)
        .astype(jnp.bfloat16)
    )
    gradient_values = (
        summed_total[:, :, HEAD_SIZE:]
        .reshape(segment_length, KEY_VALUE_HEADS * HEAD_SIZE)
        .astype(jnp.bfloat16)
    )
    return (attended, query_grad, gradient_keys, gradient_values)


def solution(mesh):
    devices = mesh.devices
    cores = 2
    fine_mesh = Mesh(
        devices.reshape(devices.shape[0], devices.shape[1] // cores, cores), ("uly", "chip", "core")
    )
    rows = P(("uly", "chip", "core"), None)
    in_specs = (rows, rows, rows, rows, P("uly", None, None))
    out_specs = (rows, rows, rows, rows)
    return jax.shard_map(body, mesh=fine_mesh, in_specs=in_specs, out_specs=out_specs, check_vma=False)
```

```python
import functools
import math

import jax
import jax.numpy as jnp
from jax import lax
from jax.experimental import pallas as pl
from jax.experimental.pallas import tpu as pltpu
from jax.sharding import Mesh, PartitionSpec as P

KEY_VALUE_HEADS = 2
HEAD_SIZE = 128
BLOCK = 128


def attention_kernel(
    tab_ref, q_ref, g_ref, pq_ref, pg_ref, kv_ref, out_ref, dq_ref, dkv_ref, kvg_ref,
    *, heads_dev, slots, seg_len, list_len, units_per_block, score_scale,
):
    dkv_ref[...] = jnp.zeros(dkv_ref.shape, jnp.float32)
    n_items = 2 * heads_dev * slots
    key_len = list_len * BLOCK
    base_at = n_items
    rows_at = n_items + n_items * list_len
    grad_at = rows_at + n_items * list_len * units_per_block
    lane = lax.broadcasted_iota(jnp.int32, (1, key_len), 1)
    lane_block = lane // BLOCK
    lane_offset = lane % BLOCK
    query_offset = lax.broadcasted_iota(jnp.int32, (seg_len, 1), 0)
    nt = (((1,), (1,)), ((), ()))
    tn = (((0,), (0,)), ((), ()))
    sources = ((q_ref, g_ref, True), (pq_ref, pg_ref, False))
    for source, (sq_ref, sg_ref, own) in enumerate(sources):
      for head in range(heads_dev):
        cols = slice(head * HEAD_SIZE, (head + 1) * HEAD_SIZE)

        def item_step(slot, carry, head=head, cols=cols, source=source, sq_ref=sq_ref, sg_ref=sg_ref, own=own):
            item = (source * heads_dev + head) * slots + slot
            rows = pl.ds(pl.multiple_of(slot * seg_len, seg_len), seg_len)
            query_block = sq_ref[rows, cols]
            grad_block = sg_ref[rows, cols]
            key_pos = lane_offset
            base = jnp.zeros((1, key_len), jnp.int32)
            for j in range(list_len):
                base = jnp.where(lane_block == j, tab_ref[base_at + item * list_len + j], base)
                for u in range(units_per_block):
                    src = tab_ref[rows_at + (item * list_len + j) * units_per_block + u]
                    kvg_ref[pl.ds(j * BLOCK + u * seg_len, seg_len), :] = kv_ref[
                        pl.ds(pl.multiple_of(src, seg_len), seg_len), :
                    ]
            key_pos = base + lane_offset
            query_pos = tab_ref[item] + query_offset
            allowed = key_pos <= query_pos
            key_group = kvg_ref[:, :HEAD_SIZE]
            value_group = kvg_ref[:, HEAD_SIZE:]
            scores = (
                lax.dot_general(query_block, key_group, nt, preferred_element_type=jnp.float32)
                * score_scale
            )
            masked = jnp.where(allowed, scores, -1e30)
            row_max = jnp.max(masked, axis=1, keepdims=True)
            row_sum = jnp.sum(
                jnp.where(allowed, jnp.exp(masked - row_max), 0.0), axis=1, keepdims=True
            )
            log_sum = row_max + jnp.log(row_sum)
            weights = jnp.where(allowed, jnp.exp(masked - log_sum), 0.0)
            weights_low = weights.astype(jnp.bfloat16)
            out_block = jnp.dot(
                weights_low, value_group, preferred_element_type=jnp.float32
            ).astype(jnp.bfloat16)
            if own:
                out_ref[rows, cols] = out_block
            row_dot = jnp.sum(
                grad_block.astype(jnp.float32) * out_block.astype(jnp.float32),
                axis=1,
                keepdims=True,
            )
            grad_weights = lax.dot_general(
                grad_block, value_group, nt, preferred_element_type=jnp.float32
            )
            score_grad = (weights * (grad_weights - row_dot) * score_scale).astype(jnp.bfloat16)
            if own:
                dq_ref[rows, cols] = jnp.dot(
                    score_grad, key_group, preferred_element_type=jnp.float32
                ).astype(jnp.bfloat16)
            key_part = lax.dot_general(score_grad, query_block, tn, preferred_element_type=jnp.float32)
            value_part = lax.dot_general(weights_low, grad_block, tn, preferred_element_type=jnp.float32)
            for j in range(list_len):
                for u in range(units_per_block):
                    dst = tab_ref[grad_at + (item * list_len + j) * units_per_block + u]
                    dst_rows = pl.ds(pl.multiple_of(jnp.maximum(dst, 0), seg_len), seg_len)
                    lo = j * BLOCK + u * seg_len
                    key_rows = key_part[lo : lo + seg_len]
                    value_rows = value_part[lo : lo + seg_len]

                    @pl.when(dst >= 0)
                    def _(dst_rows=dst_rows, key_rows=key_rows, value_rows=value_rows):
                        dkv_ref[dst_rows, :HEAD_SIZE] += key_rows
                        dkv_ref[dst_rows, HEAD_SIZE:] += value_rows
            return carry

        lax.fori_loop(0, slots, item_step, 0)


def body(queries, key_vector_rows, value_vector_rows, out_grad, block_list):
    ulysses_width = lax.axis_size("uly")
    core_count = lax.axis_size("core")
    chip_count = lax.axis_size("chip")
    cycle_size = chip_count * core_count
    segment_length = queries.shape[0]
    heads_dev = block_list.shape[0]
    list_len = block_list.shape[2]
    head_width = heads_dev * HEAD_SIZE
    copy_count = ulysses_width // KEY_VALUE_HEADS
    core_index = lax.axis_index("core")
    cycle_index = lax.axis_index("chip") * core_count + core_index
    score_scale = 1.0 / math.sqrt(HEAD_SIZE)
    sub_length = min(segment_length, BLOCK)
    sub_count = segment_length // sub_length
    unit_len = min(segment_length, BLOCK)
    units_per_block = BLOCK // unit_len
    units_per_segment = segment_length // unit_len
    total_tokens = segment_length * ulysses_width * cycle_size
    units_total = total_tokens // unit_len
    query_slots = queries.reshape(segment_length, ulysses_width, head_width)
    grad_slots = out_grad.reshape(segment_length, ulysses_width, head_width)
    kv_local = jnp.concatenate(
        [
            key_vector_rows.reshape(segment_length, KEY_VALUE_HEADS, HEAD_SIZE),
            value_vector_rows.reshape(segment_length, KEY_VALUE_HEADS, HEAD_SIZE),
        ],
        axis=2,
    )
    kv_slots = jnp.repeat(kv_local, copy_count, axis=1)
    query_all, kv_mine, grad_all = (
        lax.all_to_all(query_slots, "uly", split_axis=1, concat_axis=0, tiled=True),
        lax.all_to_all(kv_slots, "uly", split_axis=1, concat_axis=0, tiled=True),
        lax.all_to_all(grad_slots, "uly", split_axis=1, concat_axis=0, tiled=True),
    )
    keys_all = lax.all_gather(kv_mine[:, 0, :], ("chip", "core"), axis=0, tiled=True)
    item_count = heads_dev * ulysses_width
    item_ids = jnp.arange(item_count, dtype=jnp.int32)
    head_ids = item_ids // ulysses_width
    slot_ids = item_ids % ulysses_width
    earlier = jnp.arange(list_len)[:, None] > jnp.arange(list_len)[None, :]
    units_per_block = BLOCK // segment_length
    chip_index = lax.axis_index("chip")

    def item_table(source_core):
        first_pos = (slot_ids * cycle_size + chip_index * core_count + source_core) * segment_length
        entries = block_list[head_ids, first_pos // BLOCK]
        repeated = jnp.any(
            (entries[:, :, None] == entries[:, None, :]) & earlier[None, :, :], axis=2
        )
        key_base = jnp.where(repeated, 1 << 30, entries * BLOCK)
        natural_segs = (
            entries[:, :, None] * units_per_block
            + jnp.arange(units_per_block, dtype=jnp.int32)[None, None, :]
        )
        canon_rows = (
            natural_segs % cycle_size * ulysses_width + natural_segs // cycle_size
        ) * segment_length
        seg_owner = natural_segs % cycle_size
        grad_rows = jnp.where(
            seg_owner % core_count == core_index,
            (seg_owner // core_count * ulysses_width + natural_segs // cycle_size) * segment_length,
            -1,
        )
        return first_pos, key_base, canon_rows, grad_rows

    mine = item_table(core_index)
    peer = item_table(1 - core_index)
    table = jnp.concatenate(
        [jnp.concatenate([a.reshape(-1), b.reshape(-1)]) for a, b in zip(mine, peer)]
    ).astype(jnp.int32)
    q_rows = query_all.reshape(ulysses_width * segment_length, head_width)
    g_rows = grad_all.reshape(ulysses_width * segment_length, head_width)
    pair = [(0, 1), (1, 0)]
    peer_q, peer_g = lax.ppermute((q_rows, g_rows), "core", pair)
    kernel = functools.partial(
        attention_kernel,
        heads_dev=heads_dev,
        slots=ulysses_width,
        seg_len=segment_length,
        list_len=list_len,
        units_per_block=units_per_block,
        score_scale=score_scale,
    )
    out_rows, qgrad_rows, kv_grad_all = pl.pallas_call(
        kernel,
        out_shape=(
            jax.ShapeDtypeStruct(q_rows.shape, jnp.bfloat16),
            jax.ShapeDtypeStruct(q_rows.shape, jnp.bfloat16),
            jax.ShapeDtypeStruct(
                (keys_all.shape[0] // core_count, keys_all.shape[1]), jnp.float32
            ),
        ),
        in_specs=[pl.BlockSpec(memory_space=pltpu.SMEM)]
        + [pl.BlockSpec(memory_space=pltpu.VMEM)] * 5,
        out_specs=(
            pl.BlockSpec(memory_space=pltpu.VMEM),
            pl.BlockSpec(memory_space=pltpu.VMEM),
            pl.BlockSpec(memory_space=pltpu.VMEM),
        ),
        scratch_shapes=[pltpu.VMEM((list_len * BLOCK, 2 * HEAD_SIZE), jnp.bfloat16)],
        compiler_params=pltpu.CompilerParams(vmem_limit_bytes=48 * 1024 * 1024),
    )(table, q_rows, g_rows, peer_q, peer_g, keys_all)
    out_items = out_rows.reshape(ulysses_width * segment_length, 1, head_width)
    qgrad_items = qgrad_rows.reshape(ulysses_width * segment_length, 1, head_width)
    attended_back, qgrad_back = (
        lax.all_to_all(out_items, "uly", split_axis=0, concat_axis=1, tiled=True),
        lax.all_to_all(qgrad_items, "uly", split_axis=0, concat_axis=1, tiled=True),
    )
    attended = attended_back.reshape(segment_length, ulysses_width * head_width)
    query_grad = qgrad_back.reshape(segment_length, ulysses_width * head_width)
    chip_part = kv_grad_all.reshape(chip_count, ulysses_width * segment_length, 2 * HEAD_SIZE)
    owned = lax.psum_scatter(chip_part, "chip", scatter_dimension=0, tiled=True)
    by_source = lax.all_to_all(
        owned.reshape(ulysses_width, segment_length, 2 * HEAD_SIZE),
        "uly",
        split_axis=0,
        concat_axis=0,
        tiled=True,
    )
    summed_total = (
        by_source.reshape(KEY_VALUE_HEADS, copy_count, segment_length, 2 * HEAD_SIZE)
        .sum(axis=1)
        .transpose(1, 0, 2)
    )
    gradient_keys = (
        summed_total[:, :, :HEAD_SIZE]
        .reshape(segment_length, KEY_VALUE_HEADS * HEAD_SIZE)
        .astype(jnp.bfloat16)
    )
    gradient_values = (
        summed_total[:, :, HEAD_SIZE:]
        .reshape(segment_length, KEY_VALUE_HEADS * HEAD_SIZE)
        .astype(jnp.bfloat16)
    )
    return (attended, query_grad, gradient_keys, gradient_values)


def solution(mesh):
    devices = mesh.devices
    cores = 2
    fine_mesh = Mesh(
        devices.reshape(devices.shape[0], devices.shape[1] // cores, cores), ("uly", "chip", "core")
    )
    rows = P(("uly", "chip", "core"), None)
    in_specs = (rows, rows, rows, rows, P("uly", None, None))
    out_specs = (rows, rows, rows, rows)
    return jax.shard_map(body, mesh=fine_mesh, in_specs=in_specs, out_specs=out_specs, check_vma=False)
```

```python
import functools
import math

import jax
import jax.numpy as jnp
from jax import lax
from jax.experimental import pallas as pl
from jax.experimental.pallas import tpu as pltpu
from jax.sharding import Mesh, PartitionSpec as P

KEY_VALUE_HEADS = 2
HEAD_SIZE = 128
BLOCK = 128


def attention_kernel(
    tab_ref, q_ref, g_ref, pq_ref, pg_ref, kv_ref, out_ref, dq_ref, dkv_ref, kvg_ref,
    *, heads_dev, slots, seg_len, list_len, units_per_block, score_scale,
):
    dkv_ref[...] = jnp.zeros(dkv_ref.shape, jnp.float32)
    n_items = 2 * heads_dev * slots
    key_len = list_len * BLOCK
    base_at = n_items
    rows_at = n_items + n_items * list_len
    grad_at = rows_at + n_items * list_len * units_per_block
    lane = lax.broadcasted_iota(jnp.int32, (1, key_len), 1)
    lane_block = lane // BLOCK
    lane_offset = lane % BLOCK
    query_offset = lax.broadcasted_iota(jnp.int32, (seg_len, 1), 0)
    nt = (((1,), (1,)), ((), ()))
    tn = (((0,), (0,)), ((), ()))
    sources = ((q_ref, g_ref, True), (pq_ref, pg_ref, False))
    for source, (sq_ref, sg_ref, own) in enumerate(sources):
      for head in range(heads_dev):
        cols = slice(head * HEAD_SIZE, (head + 1) * HEAD_SIZE)

        def item_step(slot, carry, head=head, cols=cols, source=source, sq_ref=sq_ref, sg_ref=sg_ref, own=own):
            item = (source * heads_dev + head) * slots + slot
            rows = pl.ds(pl.multiple_of(slot * seg_len, seg_len), seg_len)
            query_block = sq_ref[rows, cols]
            grad_block = sg_ref[rows, cols]
            key_pos = lane_offset
            base = jnp.zeros((1, key_len), jnp.int32)
            for j in range(list_len):
                base = jnp.where(lane_block == j, tab_ref[base_at + item * list_len + j], base)
                for u in range(units_per_block):
                    src = tab_ref[rows_at + (item * list_len + j) * units_per_block + u]
                    kvg_ref[pl.ds(j * BLOCK + u * seg_len, seg_len), :] = kv_ref[
                        pl.ds(pl.multiple_of(src, seg_len), seg_len), :
                    ]
            key_pos = base + lane_offset
            query_pos = tab_ref[item] + query_offset
            allowed = key_pos <= query_pos
            key_group = kvg_ref[:, :HEAD_SIZE]
            value_group = kvg_ref[:, HEAD_SIZE:]
            scores = (
                lax.dot_general(query_block, key_group, nt, preferred_element_type=jnp.float32)
                * score_scale
            )
            masked = jnp.where(allowed, scores, -1e30)
            row_max = jnp.max(masked, axis=1, keepdims=True)
            row_sum = jnp.sum(
                jnp.where(allowed, jnp.exp(masked - row_max), 0.0), axis=1, keepdims=True
            )
            log_sum = row_max + jnp.log(row_sum)
            weights = jnp.where(allowed, jnp.exp(masked - log_sum), 0.0)
            weights_low = weights.astype(jnp.bfloat16)
            out_block = jnp.dot(
                weights_low, value_group, preferred_element_type=jnp.float32
            ).astype(jnp.bfloat16)
            if own:
                out_ref[rows, cols] = out_block
            row_dot = jnp.sum(
                grad_block.astype(jnp.float32) * out_block.astype(jnp.float32),
                axis=1,
                keepdims=True,
            )
            grad_weights = lax.dot_general(
                grad_block, value_group, nt, preferred_element_type=jnp.float32
            )
            score_grad = (weights * (grad_weights - row_dot) * score_scale).astype(jnp.bfloat16)
            if own:
                dq_ref[rows, cols] = jnp.dot(
                    score_grad, key_group, preferred_element_type=jnp.float32
                ).astype(jnp.bfloat16)
            key_part = lax.dot_general(score_grad, query_block, tn, preferred_element_type=jnp.float32)
            value_part = lax.dot_general(weights_low, grad_block, tn, preferred_element_type=jnp.float32)
            for j in range(list_len):
                for u in range(units_per_block):
                    dst = tab_ref[grad_at + (item * list_len + j) * units_per_block + u]
                    dst_rows = pl.ds(pl.multiple_of(jnp.maximum(dst, 0), seg_len), seg_len)
                    lo = j * BLOCK + u * seg_len
                    key_rows = key_part[lo : lo + seg_len]
                    value_rows = value_part[lo : lo + seg_len]

                    @pl.when(dst >= 0)
                    def _(dst_rows=dst_rows, key_rows=key_rows, value_rows=value_rows):
                        dkv_ref[dst_rows, :HEAD_SIZE] += key_rows
                        dkv_ref[dst_rows, HEAD_SIZE:] += value_rows
            return carry

        lax.fori_loop(0, slots, item_step, 0)


def body(queries, key_vector_rows, value_vector_rows, out_grad, block_list):
    ulysses_width = lax.axis_size("uly")
    core_count = lax.axis_size("core")
    chip_count = lax.axis_size("chip")
    cycle_size = chip_count * core_count
    segment_length = queries.shape[0]
    heads_dev = block_list.shape[0]
    list_len = block_list.shape[2]
    head_width = heads_dev * HEAD_SIZE
    copy_count = ulysses_width // KEY_VALUE_HEADS
    core_index = lax.axis_index("core")
    cycle_index = lax.axis_index("chip") * core_count + core_index
    score_scale = 1.0 / math.sqrt(HEAD_SIZE)
    sub_length = min(segment_length, BLOCK)
    sub_count = segment_length // sub_length
    unit_len = min(segment_length, BLOCK)
    units_per_block = BLOCK // unit_len
    units_per_segment = segment_length // unit_len
    total_tokens = segment_length * ulysses_width * cycle_size
    units_total = total_tokens // unit_len
    query_slots = queries.reshape(segment_length, ulysses_width, head_width)
    grad_slots = out_grad.reshape(segment_length, ulysses_width, head_width)
    kv_local = jnp.concatenate(
        [
            key_vector_rows.reshape(segment_length, KEY_VALUE_HEADS, HEAD_SIZE),
            value_vector_rows.reshape(segment_length, KEY_VALUE_HEADS, HEAD_SIZE),
        ],
        axis=2,
    )
    uly_index = lax.axis_index("uly")
    group_of = lambda u: u // copy_count
    kv_shifted = [lax.dynamic_index_in_dim(kv_local, group_of(uly_index), axis=1, keepdims=False)]
    for shift in range(1, ulysses_width):
        dest_group = group_of((uly_index + shift) % ulysses_width)
        outgoing = lax.dynamic_index_in_dim(kv_local, dest_group, axis=1, keepdims=False)
        kv_shifted.append(
            lax.ppermute(
                outgoing,
                "uly",
                [(u, (u + shift) % ulysses_width) for u in range(ulysses_width)],
            )
        )
    kv_stack = jnp.stack(kv_shifted)
    kv_mine = kv_stack[(uly_index - jnp.arange(ulysses_width)) % ulysses_width]
    query_all, grad_all = (
        lax.all_to_all(query_slots, "uly", split_axis=1, concat_axis=0, tiled=True),
        lax.all_to_all(grad_slots, "uly", split_axis=1, concat_axis=0, tiled=True),
    )
    keys_all = lax.all_gather(
        kv_mine.reshape(ulysses_width * segment_length, 2 * HEAD_SIZE), ("chip", "core"), axis=0, tiled=True
    )
    item_count = heads_dev * ulysses_width
    item_ids = jnp.arange(item_count, dtype=jnp.int32)
    head_ids = item_ids // ulysses_width
    slot_ids = item_ids % ulysses_width
    earlier = jnp.arange(list_len)[:, None] > jnp.arange(list_len)[None, :]
    units_per_block = BLOCK // segment_length
    chip_index = lax.axis_index("chip")

    def item_table(source_core):
        first_pos = (slot_ids * cycle_size + chip_index * core_count + source_core) * segment_length
        entries = block_list[head_ids, first_pos // BLOCK]
        repeated = jnp.any(
            (entries[:, :, None] == entries[:, None, :]) & earlier[None, :, :], axis=2
        )
        key_base = jnp.where(repeated, 1 << 30, entries * BLOCK)
        natural_segs = (
            entries[:, :, None] * units_per_block
            + jnp.arange(units_per_block, dtype=jnp.int32)[None, None, :]
        )
        canon_rows = (
            natural_segs % cycle_size * ulysses_width + natural_segs // cycle_size
        ) * segment_length
        seg_owner = natural_segs % cycle_size
        grad_rows = jnp.where(
            seg_owner % core_count == core_index,
            (seg_owner // core_count * ulysses_width + natural_segs // cycle_size) * segment_length,
            -1,
        )
        return first_pos, key_base, canon_rows, grad_rows

    mine = item_table(core_index)
    peer = item_table(1 - core_index)
    table = jnp.concatenate(
        [jnp.concatenate([a.reshape(-1), b.reshape(-1)]) for a, b in zip(mine, peer)]
    ).astype(jnp.int32)
    q_rows = query_all.reshape(ulysses_width * segment_length, head_width)
    g_rows = grad_all.reshape(ulysses_width * segment_length, head_width)
    pair = [(0, 1), (1, 0)]
    peer_q, peer_g = lax.ppermute((q_rows, g_rows), "core", pair)
    kernel = functools.partial(
        attention_kernel,
        heads_dev=heads_dev,
        slots=ulysses_width,
        seg_len=segment_length,
        list_len=list_len,
        units_per_block=units_per_block,
        score_scale=score_scale,
    )
    out_rows, qgrad_rows, kv_grad_all = pl.pallas_call(
        kernel,
        out_shape=(
            jax.ShapeDtypeStruct(q_rows.shape, jnp.bfloat16),
            jax.ShapeDtypeStruct(q_rows.shape, jnp.bfloat16),
            jax.ShapeDtypeStruct(
                (keys_all.shape[0] // core_count, keys_all.shape[1]), jnp.float32
            ),
        ),
        in_specs=[pl.BlockSpec(memory_space=pltpu.SMEM)]
        + [pl.BlockSpec(memory_space=pltpu.VMEM)] * 5,
        out_specs=(
            pl.BlockSpec(memory_space=pltpu.VMEM),
            pl.BlockSpec(memory_space=pltpu.VMEM),
            pl.BlockSpec(memory_space=pltpu.VMEM),
        ),
        scratch_shapes=[pltpu.VMEM((list_len * BLOCK, 2 * HEAD_SIZE), jnp.bfloat16)],
        compiler_params=pltpu.CompilerParams(vmem_limit_bytes=48 * 1024 * 1024),
    )(table, q_rows, g_rows, peer_q, peer_g, keys_all)
    out_items = out_rows.reshape(ulysses_width * segment_length, 1, head_width)
    qgrad_items = qgrad_rows.reshape(ulysses_width * segment_length, 1, head_width)
    attended_back, qgrad_back = (
        lax.all_to_all(out_items, "uly", split_axis=0, concat_axis=1, tiled=True),
        lax.all_to_all(qgrad_items, "uly", split_axis=0, concat_axis=1, tiled=True),
    )
    attended = attended_back.reshape(segment_length, ulysses_width * head_width)
    query_grad = qgrad_back.reshape(segment_length, ulysses_width * head_width)
    chip_part = kv_grad_all.reshape(chip_count, ulysses_width * segment_length, 2 * HEAD_SIZE)
    owned = lax.psum_scatter(chip_part, "chip", scatter_dimension=0, tiled=True)
    by_source = lax.all_to_all(
        owned.reshape(ulysses_width, segment_length, 2 * HEAD_SIZE),
        "uly",
        split_axis=0,
        concat_axis=0,
        tiled=True,
    )
    summed_total = (
        by_source.reshape(KEY_VALUE_HEADS, copy_count, segment_length, 2 * HEAD_SIZE)
        .sum(axis=1)
        .transpose(1, 0, 2)
    )
    gradient_keys = (
        summed_total[:, :, :HEAD_SIZE]
        .reshape(segment_length, KEY_VALUE_HEADS * HEAD_SIZE)
        .astype(jnp.bfloat16)
    )
    gradient_values = (
        summed_total[:, :, HEAD_SIZE:]
        .reshape(segment_length, KEY_VALUE_HEADS * HEAD_SIZE)
        .astype(jnp.bfloat16)
    )
    return (attended, query_grad, gradient_keys, gradient_values)


def solution(mesh):
    devices = mesh.devices
    cores = 2
    fine_mesh = Mesh(
        devices.reshape(devices.shape[0], devices.shape[1] // cores, cores), ("uly", "chip", "core")
    )
    rows = P(("uly", "chip", "core"), None)
    in_specs = (rows, rows, rows, rows, P("uly", None, None))
    out_specs = (rows, rows, rows, rows)
    return jax.shard_map(body, mesh=fine_mesh, in_specs=in_specs, out_specs=out_specs, check_vma=False)
```

```python
import functools
import math

import jax
import jax.numpy as jnp
from jax import lax
from jax.experimental import pallas as pl
from jax.experimental.pallas import tpu as pltpu
from jax.sharding import Mesh, PartitionSpec as P

KEY_VALUE_HEADS = 2
HEAD_SIZE = 128
BLOCK = 128


def attention_kernel(
    tab_ref, q_ref, g_ref, pq_ref, pg_ref, kv_ref, out_ref, dq_ref, dkv_ref, kvg_ref,
    *, heads_dev, slots, seg_len, list_len, units_per_block, score_scale,
):
    dkv_ref[...] = jnp.zeros(dkv_ref.shape, jnp.float32)
    n_items = 2 * heads_dev * slots
    key_len = list_len * BLOCK
    base_at = n_items
    rows_at = n_items + n_items * list_len
    grad_at = rows_at + n_items * list_len * units_per_block
    lane = lax.broadcasted_iota(jnp.int32, (1, key_len), 1)
    lane_block = lane // BLOCK
    lane_offset = lane % BLOCK
    query_offset = lax.broadcasted_iota(jnp.int32, (seg_len, 1), 0)
    nt = (((1,), (1,)), ((), ()))
    tn = (((0,), (0,)), ((), ()))
    sources = ((q_ref, g_ref, True), (pq_ref, pg_ref, False))
    for source, (sq_ref, sg_ref, own) in enumerate(sources):
      for head in range(heads_dev):
        cols = slice(head * HEAD_SIZE, (head + 1) * HEAD_SIZE)

        def item_step(slot, carry, head=head, cols=cols, source=source, sq_ref=sq_ref, sg_ref=sg_ref, own=own):
            item = (source * heads_dev + head) * slots + slot
            rows = pl.ds(pl.multiple_of(slot * seg_len, seg_len), seg_len)
            query_block = sq_ref[rows, cols]
            grad_block = sg_ref[rows, cols]
            key_pos = lane_offset
            base = jnp.zeros((1, key_len), jnp.int32)
            for j in range(list_len):
                base = jnp.where(lane_block == j, tab_ref[base_at + item * list_len + j], base)
                for u in range(units_per_block):
                    src = tab_ref[rows_at + (item * list_len + j) * units_per_block + u]
                    kvg_ref[pl.ds(j * BLOCK + u * seg_len, seg_len), :] = kv_ref[
                        pl.ds(pl.multiple_of(src, seg_len), seg_len), :
                    ]
            key_pos = base + lane_offset
            query_pos = tab_ref[item] + query_offset
            allowed = key_pos <= query_pos
            key_group = kvg_ref[:, :HEAD_SIZE]
            value_group = kvg_ref[:, HEAD_SIZE:]
            scores = (
                lax.dot_general(query_block, key_group, nt, preferred_element_type=jnp.float32)
                * score_scale
            )
            masked = jnp.where(allowed, scores, -1e30)
            row_max = jnp.max(masked, axis=1, keepdims=True)
            shifted = jnp.where(allowed, jnp.exp(masked - row_max), 0.0)
            row_sum = jnp.sum(shifted, axis=1, keepdims=True)
            weights = shifted / row_sum
            weights_low = weights.astype(jnp.bfloat16)
            out_block = jnp.dot(
                weights_low, value_group, preferred_element_type=jnp.float32
            ).astype(jnp.bfloat16)
            if own:
                out_ref[rows, cols] = out_block
            row_dot = jnp.sum(
                grad_block.astype(jnp.float32) * out_block.astype(jnp.float32),
                axis=1,
                keepdims=True,
            )
            grad_weights = lax.dot_general(
                grad_block, value_group, nt, preferred_element_type=jnp.float32
            )
            score_grad = (weights * (grad_weights - row_dot) * score_scale).astype(jnp.bfloat16)
            if own:
                dq_ref[rows, cols] = jnp.dot(
                    score_grad, key_group, preferred_element_type=jnp.float32
                ).astype(jnp.bfloat16)
            key_part = lax.dot_general(score_grad, query_block, tn, preferred_element_type=jnp.float32)
            value_part = lax.dot_general(weights_low, grad_block, tn, preferred_element_type=jnp.float32)
            for j in range(list_len):
                for u in range(units_per_block):
                    dst = tab_ref[grad_at + (item * list_len + j) * units_per_block + u]
                    dst_rows = pl.ds(pl.multiple_of(jnp.maximum(dst, 0), seg_len), seg_len)
                    lo = j * BLOCK + u * seg_len
                    key_rows = key_part[lo : lo + seg_len]
                    value_rows = value_part[lo : lo + seg_len]

                    @pl.when(dst >= 0)
                    def _(dst_rows=dst_rows, key_rows=key_rows, value_rows=value_rows):
                        dkv_ref[dst_rows, :HEAD_SIZE] += key_rows
                        dkv_ref[dst_rows, HEAD_SIZE:] += value_rows
            return carry

        lax.fori_loop(0, slots, item_step, 0)


def body(queries, key_vector_rows, value_vector_rows, out_grad, block_list):
    ulysses_width = lax.axis_size("uly")
    core_count = lax.axis_size("core")
    chip_count = lax.axis_size("chip")
    cycle_size = chip_count * core_count
    segment_length = queries.shape[0]
    heads_dev = block_list.shape[0]
    list_len = block_list.shape[2]
    head_width = heads_dev * HEAD_SIZE
    copy_count = ulysses_width // KEY_VALUE_HEADS
    core_index = lax.axis_index("core")
    cycle_index = lax.axis_index("chip") * core_count + core_index
    score_scale = 1.0 / math.sqrt(HEAD_SIZE)
    sub_length = min(segment_length, BLOCK)
    sub_count = segment_length // sub_length
    unit_len = min(segment_length, BLOCK)
    units_per_block = BLOCK // unit_len
    units_per_segment = segment_length // unit_len
    total_tokens = segment_length * ulysses_width * cycle_size
    units_total = total_tokens // unit_len
    query_slots = queries.reshape(segment_length, ulysses_width, head_width)
    grad_slots = out_grad.reshape(segment_length, ulysses_width, head_width)
    kv_local = jnp.concatenate(
        [
            key_vector_rows.reshape(segment_length, KEY_VALUE_HEADS, HEAD_SIZE),
            value_vector_rows.reshape(segment_length, KEY_VALUE_HEADS, HEAD_SIZE),
        ],
        axis=2,
    )
    kv_slots = jnp.repeat(kv_local, copy_count, axis=1)
    query_all, kv_mine, grad_all = (
        lax.all_to_all(query_slots, "uly", split_axis=1, concat_axis=0, tiled=True),
        lax.all_to_all(kv_slots, "uly", split_axis=1, concat_axis=0, tiled=True),
        lax.all_to_all(grad_slots, "uly", split_axis=1, concat_axis=0, tiled=True),
    )
    keys_all = lax.all_gather(kv_mine[:, 0, :], ("chip", "core"), axis=0, tiled=True)
    item_count = heads_dev * ulysses_width
    item_ids = jnp.arange(item_count, dtype=jnp.int32)
    head_ids = item_ids // ulysses_width
    slot_ids = item_ids % ulysses_width
    earlier = jnp.arange(list_len)[:, None] > jnp.arange(list_len)[None, :]
    units_per_block = BLOCK // segment_length
    chip_index = lax.axis_index("chip")

    def item_table(source_core):
        first_pos = (slot_ids * cycle_size + chip_index * core_count + source_core) * segment_length
        entries = block_list[head_ids, first_pos // BLOCK]
        repeated = jnp.any(
            (entries[:, :, None] == entries[:, None, :]) & earlier[None, :, :], axis=2
        )
        key_base = jnp.where(repeated, 1 << 30, entries * BLOCK)
        natural_segs = (
            entries[:, :, None] * units_per_block
            + jnp.arange(units_per_block, dtype=jnp.int32)[None, None, :]
        )
        canon_rows = (
            natural_segs % cycle_size * ulysses_width + natural_segs // cycle_size
        ) * segment_length
        seg_owner = natural_segs % cycle_size
        grad_rows = jnp.where(
            seg_owner % core_count == core_index,
            (seg_owner // core_count * ulysses_width + natural_segs // cycle_size) * segment_length,
            -1,
        )
        return first_pos, key_base, canon_rows, grad_rows

    mine = item_table(core_index)
    peer = item_table(1 - core_index)
    table = jnp.concatenate(
        [jnp.concatenate([a.reshape(-1), b.reshape(-1)]) for a, b in zip(mine, peer)]
    ).astype(jnp.int32)
    q_rows = query_all.reshape(ulysses_width * segment_length, head_width)
    g_rows = grad_all.reshape(ulysses_width * segment_length, head_width)
    pair = [(0, 1), (1, 0)]
    peer_q, peer_g = lax.ppermute((q_rows, g_rows), "core", pair)
    kernel = functools.partial(
        attention_kernel,
        heads_dev=heads_dev,
        slots=ulysses_width,
        seg_len=segment_length,
        list_len=list_len,
        units_per_block=units_per_block,
        score_scale=score_scale,
    )
    out_rows, qgrad_rows, kv_grad_all = pl.pallas_call(
        kernel,
        out_shape=(
            jax.ShapeDtypeStruct(q_rows.shape, jnp.bfloat16),
            jax.ShapeDtypeStruct(q_rows.shape, jnp.bfloat16),
            jax.ShapeDtypeStruct(
                (keys_all.shape[0] // core_count, keys_all.shape[1]), jnp.float32
            ),
        ),
        in_specs=[pl.BlockSpec(memory_space=pltpu.SMEM)]
        + [pl.BlockSpec(memory_space=pltpu.VMEM)] * 5,
        out_specs=(
            pl.BlockSpec(memory_space=pltpu.VMEM),
            pl.BlockSpec(memory_space=pltpu.VMEM),
            pl.BlockSpec(memory_space=pltpu.VMEM),
        ),
        scratch_shapes=[pltpu.VMEM((list_len * BLOCK, 2 * HEAD_SIZE), jnp.bfloat16)],
        compiler_params=pltpu.CompilerParams(vmem_limit_bytes=48 * 1024 * 1024),
    )(table, q_rows, g_rows, peer_q, peer_g, keys_all)
    out_items = out_rows.reshape(ulysses_width * segment_length, 1, head_width)
    qgrad_items = qgrad_rows.reshape(ulysses_width * segment_length, 1, head_width)
    attended_back, qgrad_back = (
        lax.all_to_all(out_items, "uly", split_axis=0, concat_axis=1, tiled=True),
        lax.all_to_all(qgrad_items, "uly", split_axis=0, concat_axis=1, tiled=True),
    )
    attended = attended_back.reshape(segment_length, ulysses_width * head_width)
    query_grad = qgrad_back.reshape(segment_length, ulysses_width * head_width)
    chip_part = kv_grad_all.reshape(chip_count, ulysses_width * segment_length, 2 * HEAD_SIZE)
    owned = lax.psum_scatter(chip_part, "chip", scatter_dimension=0, tiled=True)
    by_source = lax.all_to_all(
        owned.reshape(ulysses_width, segment_length, 2 * HEAD_SIZE),
        "uly",
        split_axis=0,
        concat_axis=0,
        tiled=True,
    )
    summed_total = (
        by_source.reshape(KEY_VALUE_HEADS, copy_count, segment_length, 2 * HEAD_SIZE)
        .sum(axis=1)
        .transpose(1, 0, 2)
    )
    gradient_keys = (
        summed_total[:, :, :HEAD_SIZE]
        .reshape(segment_length, KEY_VALUE_HEADS * HEAD_SIZE)
        .astype(jnp.bfloat16)
    )
    gradient_values = (
        summed_total[:, :, HEAD_SIZE:]
        .reshape(segment_length, KEY_VALUE_HEADS * HEAD_SIZE)
        .astype(jnp.bfloat16)
    )
    return (attended, query_grad, gradient_keys, gradient_values)


def solution(mesh):
    devices = mesh.devices
    cores = 2
    fine_mesh = Mesh(
        devices.reshape(devices.shape[0], devices.shape[1] // cores, cores), ("uly", "chip", "core")
    )
    rows = P(("uly", "chip", "core"), None)
    in_specs = (rows, rows, rows, rows, P("uly", None, None))
    out_specs = (rows, rows, rows, rows)
    return jax.shard_map(body, mesh=fine_mesh, in_specs=in_specs, out_specs=out_specs, check_vma=False)
```

```python
import functools
import math

import jax
import jax.numpy as jnp
from jax import lax
from jax.experimental import pallas as pl
from jax.experimental.pallas import tpu as pltpu
from jax.sharding import Mesh, PartitionSpec as P

KEY_VALUE_HEADS = 2
HEAD_SIZE = 128
BLOCK = 128


def attention_kernel(
    tab_ref, q_ref, g_ref, pq_ref, pg_ref, kv_ref, out_ref, dq_ref, dkv_ref, kvg_ref,
    *, heads_dev, slots, seg_len, list_len, units_per_block, score_scale,
):
    dkv_ref[...] = jnp.zeros(dkv_ref.shape, jnp.float32)
    n_items = 2 * heads_dev * slots
    key_len = list_len * BLOCK
    base_at = n_items
    rows_at = n_items + n_items * list_len
    grad_at = rows_at + n_items * list_len * units_per_block
    lane = lax.broadcasted_iota(jnp.int32, (1, key_len), 1)
    lane_block = lane // BLOCK
    lane_offset = lane % BLOCK
    query_offset = lax.broadcasted_iota(jnp.int32, (seg_len, 1), 0)
    nt = (((1,), (1,)), ((), ()))
    tn = (((0,), (0,)), ((), ()))
    sources = ((q_ref, g_ref, True), (pq_ref, pg_ref, False))
    for source, (sq_ref, sg_ref, own) in enumerate(sources):
      for head in range(heads_dev):
        cols = slice(head * HEAD_SIZE, (head + 1) * HEAD_SIZE)

        def item_step(slot, carry, head=head, cols=cols, source=source, sq_ref=sq_ref, sg_ref=sg_ref, own=own):
            item = (source * heads_dev + head) * slots + slot
            rows = pl.ds(pl.multiple_of(slot * seg_len, seg_len), seg_len)
            query_block = sq_ref[rows, cols]
            grad_block = sg_ref[rows, cols]
            key_pos = lane_offset
            base = jnp.zeros((1, key_len), jnp.int32)
            for j in range(list_len):
                base = jnp.where(lane_block == j, tab_ref[base_at + item * list_len + j], base)
                for u in range(units_per_block):
                    src = tab_ref[rows_at + (item * list_len + j) * units_per_block + u]
                    kvg_ref[pl.ds(j * BLOCK + u * seg_len, seg_len), :] = kv_ref[
                        pl.ds(pl.multiple_of(src, seg_len), seg_len), :
                    ]
            key_pos = base + lane_offset
            query_pos = tab_ref[item] + query_offset
            allowed = key_pos <= query_pos
            key_group = kvg_ref[:, :HEAD_SIZE]
            value_group = kvg_ref[:, HEAD_SIZE:]
            scores = (
                lax.dot_general(query_block, key_group, nt, preferred_element_type=jnp.float32)
                * score_scale
            )
            masked = jnp.where(allowed, scores, -1e30)
            row_max = jnp.max(masked, axis=1, keepdims=True)
            row_sum = jnp.sum(
                jnp.where(allowed, jnp.exp(masked - row_max), 0.0), axis=1, keepdims=True
            )
            log_sum = row_max + jnp.log(row_sum)
            weights = jnp.where(allowed, jnp.exp(masked - log_sum), 0.0)
            weights_low = weights.astype(jnp.bfloat16)
            out_block = jnp.dot(
                weights_low, value_group, preferred_element_type=jnp.float32
            ).astype(jnp.bfloat16)
            if own:
                out_ref[rows, cols] = out_block
            row_dot = jnp.sum(
                grad_block.astype(jnp.float32) * out_block.astype(jnp.float32),
                axis=1,
                keepdims=True,
            )
            grad_weights = lax.dot_general(
                grad_block, value_group, nt, preferred_element_type=jnp.float32
            )
            score_grad = (weights * (grad_weights - row_dot) * score_scale).astype(jnp.bfloat16)
            if own:
                dq_ref[rows, cols] = jnp.dot(
                    score_grad, key_group, preferred_element_type=jnp.float32
                ).astype(jnp.bfloat16)
            key_part = lax.dot_general(score_grad, query_block, tn, preferred_element_type=jnp.float32)
            value_part = lax.dot_general(weights_low, grad_block, tn, preferred_element_type=jnp.float32)
            for j in range(list_len):
                for u in range(units_per_block):
                    dst = tab_ref[grad_at + (item * list_len + j) * units_per_block + u]
                    dst_rows = pl.ds(pl.multiple_of(jnp.maximum(dst, 0), seg_len), seg_len)
                    lo = j * BLOCK + u * seg_len
                    key_rows = key_part[lo : lo + seg_len]
                    value_rows = value_part[lo : lo + seg_len]

                    @pl.when(dst >= 0)
                    def _(dst_rows=dst_rows, key_rows=key_rows, value_rows=value_rows):
                        dkv_ref[dst_rows, :HEAD_SIZE] += key_rows
                        dkv_ref[dst_rows, HEAD_SIZE:] += value_rows
            return carry

        lax.fori_loop(0, slots, item_step, 0)


def body(queries, key_vector_rows, value_vector_rows, out_grad, block_list):
    ulysses_width = lax.axis_size("uly")
    core_count = lax.axis_size("core")
    chip_count = lax.axis_size("chip")
    cycle_size = chip_count * core_count
    segment_length = queries.shape[0]
    heads_dev = block_list.shape[0]
    list_len = block_list.shape[2]
    head_width = heads_dev * HEAD_SIZE
    copy_count = ulysses_width // KEY_VALUE_HEADS
    core_index = lax.axis_index("core")
    cycle_index = lax.axis_index("chip") * core_count + core_index
    score_scale = 1.0 / math.sqrt(HEAD_SIZE)
    sub_length = min(segment_length, BLOCK)
    sub_count = segment_length // sub_length
    unit_len = min(segment_length, BLOCK)
    units_per_block = BLOCK // unit_len
    units_per_segment = segment_length // unit_len
    total_tokens = segment_length * ulysses_width * cycle_size
    units_total = total_tokens // unit_len
    query_slots = queries.reshape(segment_length, ulysses_width, head_width)
    grad_slots = out_grad.reshape(segment_length, ulysses_width, head_width)
    kv_local = jnp.concatenate(
        [
            key_vector_rows.reshape(segment_length, KEY_VALUE_HEADS, HEAD_SIZE),
            value_vector_rows.reshape(segment_length, KEY_VALUE_HEADS, HEAD_SIZE),
        ],
        axis=2,
    )
    kv_slots = jnp.repeat(kv_local, copy_count, axis=1)
    kv_mine = lax.all_to_all(kv_slots, "uly", split_axis=1, concat_axis=0, tiled=True)
    both_all = lax.all_to_all(
        jnp.concatenate([query_slots, grad_slots], axis=2), "uly", split_axis=1, concat_axis=0, tiled=True
    )
    query_all = both_all[:, :, :head_width]
    grad_all = both_all[:, :, head_width:]
    keys_all = lax.all_gather(kv_mine[:, 0, :], ("chip", "core"), axis=0, tiled=True)
    item_count = heads_dev * ulysses_width
    item_ids = jnp.arange(item_count, dtype=jnp.int32)
    head_ids = item_ids // ulysses_width
    slot_ids = item_ids % ulysses_width
    earlier = jnp.arange(list_len)[:, None] > jnp.arange(list_len)[None, :]
    units_per_block = BLOCK // segment_length
    chip_index = lax.axis_index("chip")

    def item_table(source_core):
        first_pos = (slot_ids * cycle_size + chip_index * core_count + source_core) * segment_length
        entries = block_list[head_ids, first_pos // BLOCK]
        repeated = jnp.any(
            (entries[:, :, None] == entries[:, None, :]) & earlier[None, :, :], axis=2
        )
        key_base = jnp.where(repeated, 1 << 30, entries * BLOCK)
        natural_segs = (
            entries[:, :, None] * units_per_block
            + jnp.arange(units_per_block, dtype=jnp.int32)[None, None, :]
        )
        canon_rows = (
            natural_segs % cycle_size * ulysses_width + natural_segs // cycle_size
        ) * segment_length
        seg_owner = natural_segs % cycle_size
        grad_rows = jnp.where(
            seg_owner % core_count == core_index,
            (seg_owner // core_count * ulysses_width + natural_segs // cycle_size) * segment_length,
            -1,
        )
        return first_pos, key_base, canon_rows, grad_rows

    mine = item_table(core_index)
    peer = item_table(1 - core_index)
    table = jnp.concatenate(
        [jnp.concatenate([a.reshape(-1), b.reshape(-1)]) for a, b in zip(mine, peer)]
    ).astype(jnp.int32)
    q_rows = query_all.reshape(ulysses_width * segment_length, head_width)
    g_rows = grad_all.reshape(ulysses_width * segment_length, head_width)
    pair = [(0, 1), (1, 0)]
    peer_q, peer_g = lax.ppermute((q_rows, g_rows), "core", pair)
    kernel = functools.partial(
        attention_kernel,
        heads_dev=heads_dev,
        slots=ulysses_width,
        seg_len=segment_length,
        list_len=list_len,
        units_per_block=units_per_block,
        score_scale=score_scale,
    )
    out_rows, qgrad_rows, kv_grad_all = pl.pallas_call(
        kernel,
        out_shape=(
            jax.ShapeDtypeStruct(q_rows.shape, jnp.bfloat16),
            jax.ShapeDtypeStruct(q_rows.shape, jnp.bfloat16),
            jax.ShapeDtypeStruct(
                (keys_all.shape[0] // core_count, keys_all.shape[1]), jnp.float32
            ),
        ),
        in_specs=[pl.BlockSpec(memory_space=pltpu.SMEM)]
        + [pl.BlockSpec(memory_space=pltpu.VMEM)] * 5,
        out_specs=(
            pl.BlockSpec(memory_space=pltpu.VMEM),
            pl.BlockSpec(memory_space=pltpu.VMEM),
            pl.BlockSpec(memory_space=pltpu.VMEM),
        ),
        scratch_shapes=[pltpu.VMEM((list_len * BLOCK, 2 * HEAD_SIZE), jnp.bfloat16)],
        compiler_params=pltpu.CompilerParams(vmem_limit_bytes=48 * 1024 * 1024),
    )(table, q_rows, g_rows, peer_q, peer_g, keys_all)
    out_items = out_rows.reshape(ulysses_width * segment_length, 1, head_width)
    qgrad_items = qgrad_rows.reshape(ulysses_width * segment_length, 1, head_width)
    attended_back, qgrad_back = (
        lax.all_to_all(out_items, "uly", split_axis=0, concat_axis=1, tiled=True),
        lax.all_to_all(qgrad_items, "uly", split_axis=0, concat_axis=1, tiled=True),
    )
    attended = attended_back.reshape(segment_length, ulysses_width * head_width)
    query_grad = qgrad_back.reshape(segment_length, ulysses_width * head_width)
    chip_part = kv_grad_all.reshape(chip_count, ulysses_width * segment_length, 2 * HEAD_SIZE)
    owned = lax.psum_scatter(chip_part, "chip", scatter_dimension=0, tiled=True)
    by_source = lax.all_to_all(
        owned.reshape(ulysses_width, segment_length, 2 * HEAD_SIZE),
        "uly",
        split_axis=0,
        concat_axis=0,
        tiled=True,
    )
    summed_total = (
        by_source.reshape(KEY_VALUE_HEADS, copy_count, segment_length, 2 * HEAD_SIZE)
        .sum(axis=1)
        .transpose(1, 0, 2)
    )
    gradient_keys = (
        summed_total[:, :, :HEAD_SIZE]
        .reshape(segment_length, KEY_VALUE_HEADS * HEAD_SIZE)
        .astype(jnp.bfloat16)
    )
    gradient_values = (
        summed_total[:, :, HEAD_SIZE:]
        .reshape(segment_length, KEY_VALUE_HEADS * HEAD_SIZE)
        .astype(jnp.bfloat16)
    )
    return (attended, query_grad, gradient_keys, gradient_values)


def solution(mesh):
    devices = mesh.devices
    cores = 2
    fine_mesh = Mesh(
        devices.reshape(devices.shape[0], devices.shape[1] // cores, cores), ("uly", "chip", "core")
    )
    rows = P(("uly", "chip", "core"), None)
    in_specs = (rows, rows, rows, rows, P("uly", None, None))
    out_specs = (rows, rows, rows, rows)
    return jax.shard_map(body, mesh=fine_mesh, in_specs=in_specs, out_specs=out_specs, check_vma=False)
```

```python
import functools
import math

import jax
import jax.numpy as jnp
from jax import lax
from jax.experimental import pallas as pl
from jax.experimental.pallas import tpu as pltpu
from jax.sharding import Mesh, PartitionSpec as P

KEY_VALUE_HEADS = 2
HEAD_SIZE = 128
BLOCK = 128


def attention_kernel(
    tab_ref, q_ref, g_ref, pq_ref, pg_ref, kv_ref, out_ref, dq_ref, dkv_ref, kvg_ref,
    *, heads_dev, slots, seg_len, list_len, units_per_block, score_scale,
):
    dkv_ref[...] = jnp.zeros(dkv_ref.shape, jnp.float32)
    n_items = 2 * heads_dev * slots
    key_len = list_len * BLOCK
    base_at = n_items
    rows_at = n_items + n_items * list_len
    grad_at = rows_at + n_items * list_len * units_per_block
    lane = lax.broadcasted_iota(jnp.int32, (1, key_len), 1)
    lane_block = lane // BLOCK
    lane_offset = lane % BLOCK
    query_offset = lax.broadcasted_iota(jnp.int32, (seg_len, 1), 0)
    nt = (((1,), (1,)), ((), ()))
    tn = (((0,), (0,)), ((), ()))
    sources = ((q_ref, g_ref, True), (pq_ref, pg_ref, False))
    for source, (sq_ref, sg_ref, own) in enumerate(sources):
      for head in range(heads_dev):
        cols = slice(head * HEAD_SIZE, (head + 1) * HEAD_SIZE)

        def item_step(slot, carry, head=head, cols=cols, source=source, sq_ref=sq_ref, sg_ref=sg_ref, own=own):
            item = (source * heads_dev + head) * slots + slot
            rows = pl.ds(pl.multiple_of(slot * seg_len, seg_len), seg_len)
            query_block = sq_ref[rows, cols]
            grad_block = sg_ref[rows, cols]
            key_pos = lane_offset
            base = jnp.zeros((1, key_len), jnp.int32)
            for j in range(list_len):
                base = jnp.where(lane_block == j, tab_ref[base_at + item * list_len + j], base)
                for u in range(units_per_block):
                    src = tab_ref[rows_at + (item * list_len + j) * units_per_block + u]
                    kvg_ref[pl.ds(j * BLOCK + u * seg_len, seg_len), :] = kv_ref[
                        pl.ds(pl.multiple_of(src, seg_len), seg_len), :
                    ]
            key_pos = base + lane_offset
            query_pos = tab_ref[item] + query_offset
            allowed = key_pos <= query_pos
            key_group = kvg_ref[:, :HEAD_SIZE]
            value_group = kvg_ref[:, HEAD_SIZE:]
            scores = (
                lax.dot_general(query_block, key_group, nt, preferred_element_type=jnp.float32)
                * score_scale
            )
            masked = jnp.where(allowed, scores, -1e30)
            row_max = jnp.max(masked, axis=1, keepdims=True)
            row_sum = jnp.sum(
                jnp.where(allowed, jnp.exp(masked - row_max), 0.0), axis=1, keepdims=True
            )
            log_sum = row_max + jnp.log(row_sum)
            weights = jnp.where(allowed, jnp.exp(masked - log_sum), 0.0)
            weights_low = weights.astype(jnp.bfloat16)
            out_block = jnp.dot(
                weights_low, value_group, preferred_element_type=jnp.float32
            ).astype(jnp.bfloat16)
            if own:
                out_ref[rows, cols] = out_block
            row_dot = jnp.sum(
                grad_block.astype(jnp.float32) * out_block.astype(jnp.float32),
                axis=1,
                keepdims=True,
            )
            grad_weights = lax.dot_general(
                grad_block, value_group, nt, preferred_element_type=jnp.float32
            )
            score_grad = (weights * (grad_weights - row_dot) * score_scale).astype(jnp.bfloat16)
            if own:
                dq_ref[rows, cols] = jnp.dot(
                    score_grad, key_group, preferred_element_type=jnp.float32
                ).astype(jnp.bfloat16)
            key_part = lax.dot_general(score_grad, query_block, tn, preferred_element_type=jnp.float32)
            value_part = lax.dot_general(weights_low, grad_block, tn, preferred_element_type=jnp.float32)
            for j in range(list_len):
                for u in range(units_per_block):
                    dst = tab_ref[grad_at + (item * list_len + j) * units_per_block + u]
                    dst_rows = pl.ds(pl.multiple_of(jnp.maximum(dst, 0), seg_len), seg_len)
                    lo = j * BLOCK + u * seg_len
                    key_rows = key_part[lo : lo + seg_len]
                    value_rows = value_part[lo : lo + seg_len]

                    @pl.when(dst >= 0)
                    def _(dst_rows=dst_rows, key_rows=key_rows, value_rows=value_rows):
                        dkv_ref[dst_rows, :HEAD_SIZE] += key_rows
                        dkv_ref[dst_rows, HEAD_SIZE:] += value_rows
            return carry

        lax.fori_loop(0, slots, item_step, 0)


def body(queries, key_vector_rows, value_vector_rows, out_grad, block_list):
    ulysses_width = lax.axis_size("uly")
    core_count = lax.axis_size("core")
    chip_count = lax.axis_size("chip")
    cycle_size = chip_count * core_count
    segment_length = queries.shape[0]
    heads_dev = block_list.shape[0]
    list_len = block_list.shape[2]
    head_width = heads_dev * HEAD_SIZE
    copy_count = ulysses_width // KEY_VALUE_HEADS
    core_index = lax.axis_index("core")
    cycle_index = lax.axis_index("chip") * core_count + core_index
    score_scale = 1.0 / math.sqrt(HEAD_SIZE)
    sub_length = min(segment_length, BLOCK)
    sub_count = segment_length // sub_length
    unit_len = min(segment_length, BLOCK)
    units_per_block = BLOCK // unit_len
    units_per_segment = segment_length // unit_len
    total_tokens = segment_length * ulysses_width * cycle_size
    units_total = total_tokens // unit_len
    query_slots = queries.reshape(segment_length, ulysses_width, head_width)
    grad_slots = out_grad.reshape(segment_length, ulysses_width, head_width)
    kv_local = jnp.concatenate(
        [
            key_vector_rows.reshape(segment_length, KEY_VALUE_HEADS, HEAD_SIZE),
            value_vector_rows.reshape(segment_length, KEY_VALUE_HEADS, HEAD_SIZE),
        ],
        axis=2,
    )
    kv_slots = jnp.repeat(kv_local, copy_count, axis=1)
    kv_mine = lax.all_to_all(kv_slots, "uly", split_axis=1, concat_axis=0, tiled=True)
    both_all = lax.all_to_all(
        jnp.concatenate([query_slots, grad_slots], axis=2), "uly", split_axis=1, concat_axis=0, tiled=True
    )
    query_all = both_all[:, :, :head_width]
    grad_all = both_all[:, :, head_width:]
    keys_all = lax.all_gather(kv_mine[:, 0, :], ("chip", "core"), axis=0, tiled=True)
    item_count = heads_dev * ulysses_width
    item_ids = jnp.arange(item_count, dtype=jnp.int32)
    head_ids = item_ids // ulysses_width
    slot_ids = item_ids % ulysses_width
    earlier = jnp.arange(list_len)[:, None] > jnp.arange(list_len)[None, :]
    units_per_block = BLOCK // segment_length
    chip_index = lax.axis_index("chip")

    def item_table(source_core):
        first_pos = (slot_ids * cycle_size + chip_index * core_count + source_core) * segment_length
        entries = block_list[head_ids, first_pos // BLOCK]
        repeated = jnp.any(
            (entries[:, :, None] == entries[:, None, :]) & earlier[None, :, :], axis=2
        )
        key_base = jnp.where(repeated, 1 << 30, entries * BLOCK)
        natural_segs = (
            entries[:, :, None] * units_per_block
            + jnp.arange(units_per_block, dtype=jnp.int32)[None, None, :]
        )
        canon_rows = (
            natural_segs % cycle_size * ulysses_width + natural_segs // cycle_size
        ) * segment_length
        seg_owner = natural_segs % cycle_size
        grad_rows = jnp.where(
            seg_owner % core_count == core_index,
            (seg_owner // core_count * ulysses_width + natural_segs // cycle_size) * segment_length,
            -1,
        )
        return first_pos, key_base, canon_rows, grad_rows

    mine = item_table(core_index)
    peer = item_table(1 - core_index)
    table = jnp.concatenate(
        [jnp.concatenate([a.reshape(-1), b.reshape(-1)]) for a, b in zip(mine, peer)]
    ).astype(jnp.int32)
    q_rows = query_all.reshape(ulysses_width * segment_length, head_width)
    g_rows = grad_all.reshape(ulysses_width * segment_length, head_width)
    pair = [(0, 1), (1, 0)]
    peer_q, peer_g = lax.ppermute((q_rows, g_rows), "core", pair)
    kernel = functools.partial(
        attention_kernel,
        heads_dev=heads_dev,
        slots=ulysses_width,
        seg_len=segment_length,
        list_len=list_len,
        units_per_block=units_per_block,
        score_scale=score_scale,
    )
    out_rows, qgrad_rows, kv_grad_all = pl.pallas_call(
        kernel,
        out_shape=(
            jax.ShapeDtypeStruct(q_rows.shape, jnp.bfloat16),
            jax.ShapeDtypeStruct(q_rows.shape, jnp.bfloat16),
            jax.ShapeDtypeStruct(
                (keys_all.shape[0] // core_count, keys_all.shape[1]), jnp.float32
            ),
        ),
        in_specs=[pl.BlockSpec(memory_space=pltpu.SMEM)]
        + [pl.BlockSpec(memory_space=pltpu.VMEM)] * 5,
        out_specs=(
            pl.BlockSpec(memory_space=pltpu.VMEM),
            pl.BlockSpec(memory_space=pltpu.VMEM),
            pl.BlockSpec(memory_space=pltpu.VMEM),
        ),
        scratch_shapes=[pltpu.VMEM((list_len * BLOCK, 2 * HEAD_SIZE), jnp.bfloat16)],
        compiler_params=pltpu.CompilerParams(vmem_limit_bytes=48 * 1024 * 1024),
    )(table, q_rows, g_rows, peer_q, peer_g, keys_all)
    out_items = out_rows.reshape(ulysses_width * segment_length, 1, head_width)
    qgrad_items = qgrad_rows.reshape(ulysses_width * segment_length, 1, head_width)
    both_back = lax.all_to_all(
        jnp.concatenate([out_items, qgrad_items], axis=2), "uly", split_axis=0, concat_axis=1, tiled=True
    )
    attended_back = both_back[:, :, :head_width]
    qgrad_back = both_back[:, :, head_width:]
    attended = attended_back.reshape(segment_length, ulysses_width * head_width)
    query_grad = qgrad_back.reshape(segment_length, ulysses_width * head_width)
    chip_part = kv_grad_all.reshape(chip_count, ulysses_width * segment_length, 2 * HEAD_SIZE)
    owned = lax.psum_scatter(chip_part, "chip", scatter_dimension=0, tiled=True)
    by_source = lax.all_to_all(
        owned.reshape(ulysses_width, segment_length, 2 * HEAD_SIZE),
        "uly",
        split_axis=0,
        concat_axis=0,
        tiled=True,
    )
    summed_total = (
        by_source.reshape(KEY_VALUE_HEADS, copy_count, segment_length, 2 * HEAD_SIZE)
        .sum(axis=1)
        .transpose(1, 0, 2)
    )
    gradient_keys = (
        summed_total[:, :, :HEAD_SIZE]
        .reshape(segment_length, KEY_VALUE_HEADS * HEAD_SIZE)
        .astype(jnp.bfloat16)
    )
    gradient_values = (
        summed_total[:, :, HEAD_SIZE:]
        .reshape(segment_length, KEY_VALUE_HEADS * HEAD_SIZE)
        .astype(jnp.bfloat16)
    )
    return (attended, query_grad, gradient_keys, gradient_values)


def solution(mesh):
    devices = mesh.devices
    cores = 2
    fine_mesh = Mesh(
        devices.reshape(devices.shape[0], devices.shape[1] // cores, cores), ("uly", "chip", "core")
    )
    rows = P(("uly", "chip", "core"), None)
    in_specs = (rows, rows, rows, rows, P("uly", None, None))
    out_specs = (rows, rows, rows, rows)
    return jax.shard_map(body, mesh=fine_mesh, in_specs=in_specs, out_specs=out_specs, check_vma=False)
```
